512 devices in a mesh: freq: 128 (over y, z, core), tm: 4 (over x).
Axes of the slice: x: 4, y: 8, z: 8, core: 2. Of those that a mesh axis runs over, the one named last changes fastest.
Arguments:
- spectrogram: bfloat16 [65536, 2048], P('freq', 'tm'), may hold values from -6 to 6
- low_share: int32 [2047], replicated, may hold values from 24 to 44
- jitter: int32 [4094], replicated, may hold values from 0 to 63
Outputs:
- best: float32 [9, 2048], P(None, 'tm')
The draws below stay inside these ranges and needn't reach their ends.
All inputs are finite; a program needn't handle non-finite values.
Results may differ from the reference program's by a relative error of at most 0.0003.
Values sent between devices are 32-bit elements; how exact they have to be, the bound alone decides.
No kernel may reach another device: no remote copies, remote signals or barrier semaphores. Data moves between devices by JAX's collectives and lax.ppermute only.
A program may use at most 64 MiB of HBM per device.

```python
import math
import jax
import jax.numpy as jnp
from jax import lax

SUMMED = 32
WIDTHS = 9
CHANNELS = 65536
TRIALS = 2048
TIME = 2048


def with_ends(result, own_key, smallest, top_value):
    place = [jax.random.randint(jax.random.fold_in(own_key, axis), (), 0, length) for axis, length in enumerate(result.shape)]
    longest = result.shape.index(max(result.shape))
    next_to = place[:longest] + [(place[longest] + 1) % result.shape[longest]] + place[longest + 1:]
    return result.at[tuple(place)].set(smallest).at[tuple(next_to)].set(top_value)


def steps_of(rng, extent, shards, least, top_value):
    loudness = 1.0
    for dim, blocks in shards:
        heights = jax.random.uniform(jax.random.fold_in(jax.random.fold_in(rng, 6), dim), (blocks,), jnp.float32, least / len(shards), top_value / len(shards))
        loudness = loudness * jnp.repeat(jnp.exp(heights), extent[dim] // blocks).reshape((-1,) + (1,) * (len(extent) - 1 - dim))
    return loudness


def bell_draw(key, shape, deviation, bound, shards=(), kind=jnp.bfloat16):
    values = jax.random.normal(key, shape, jnp.float32) * deviation
    if len(shards) > 0:
        values = steps_of(key, shape, shards, -0.22, 0.18) * values
    return jnp.clip(values, min=-bound, max=bound).astype(kind)


def setup_inputs(seed: int = 0) -> dict:
    streams_of = jax.random.split(jax.random.key(seed), 4)
    return {
        "spectrogram": bell_draw(streams_of[0], (CHANNELS, TIME), 1.0, 6.0, ((0, 128), (1, 4))),
        "low_share": with_ends(jax.random.randint(streams_of[1], (TRIALS - 1,), 24, 45), jax.random.fold_in(streams_of[1], 1), 24, 44).astype(jnp.int32),
        "jitter": with_ends(jax.random.randint(streams_of[2], (2 * TRIALS - 2,), 0, 64), jax.random.fold_in(streams_of[2], 1), 0, 63).astype(jnp.int32),
    }


def shift_table(trial_count, low_share, jitter):
    groups = TRIALS // trial_count
    subband = jnp.arange(groups, dtype=jnp.int32)[:, None]
    trial_ids = jnp.arange(trial_count, dtype=jnp.int32)[None, :]
    rate_rows = jnp.take(low_share, groups - 1 + subband)
    return (trial_ids * rate_rows + jnp.take(jitter, trial_count - 2 + trial_ids)) // 64

def reference(spectrogram, low_share, jitter):
    states = lax.optimization_barrier(jnp.sum(spectrogram.reshape(TRIALS, SUMMED, TIME), axis=1, dtype=jnp.float32))[:, None, :]
    trial_count = 2
    while trial_count <= TRIALS:
        low_rows = jnp.repeat(states[0::2], 2, axis=1)
        high_rows = jnp.repeat(states[1::2], 2, axis=1)
        shifts = shift_table(trial_count, low_share, jitter)
        padded = jnp.pad(high_rows, ((0, 0), (0, 0), (trial_count, 0)))
        index_grid = (trial_count - shifts)[:, :, None] + jnp.arange(TIME, dtype=jnp.int32)[None, None, :]
        states = low_rows + jnp.take_along_axis(padded, index_grid, axis=2)
        trial_count = trial_count * 2
    signal = states[0] / math.sqrt(CHANNELS)
    window = signal
    outputs = []
    width_now = 1
    for level_index in range(WIDTHS):
        outputs.append(lax.optimization_barrier(jnp.max(window, axis=0)) / math.sqrt(width_now))
        window = window + jnp.pad(window, ((0, 0), (width_now, 0)))[:, :TIME]
        width_now = width_now * 2
    return jnp.stack(outputs)
```

```python
import math

import jax
import jax.numpy as jnp
from jax import lax
from jax.sharding import PartitionSpec as P

SUMMED = 32
WIDTHS = 9


def passed_along(block, axis, distance):
    devices = range(lax.axis_size(axis))
    route = [(i - distance, i) for i in devices if i - distance in devices]
    return lax.ppermute(block, axis, route)


def swapped(block, axis, apart):
    count = lax.axis_size(axis)
    route = []
    for low in range(count):
        high = low | 1 << apart
        if high != low and high < count:
            route += [(low, high), (high, low)]
    return lax.ppermute(block, axis, route)


def widen(trial_rows, fetch_width):
    if fetch_width == 0:
        return trial_rows
    span_time = trial_rows.shape[-1]
    hop_count = min(-(-fetch_width // span_time), lax.axis_size("tm") - 1)
    pieces = [trial_rows]
    fetched = 0
    for hop_index in range(1, hop_count + 1):
        taken_cols = min(span_time, fetch_width - fetched)
        arrived = passed_along(trial_rows[..., span_time - taken_cols :], "tm", hop_index)
        pieces.insert(0, arrived)
        fetched = fetched + taken_cols
    if fetched < fetch_width:
        pieces.insert(
            0, jnp.zeros(trial_rows.shape[:-1] + (fetch_width - fetched,), trial_rows.dtype)
        )
    return jnp.concatenate(pieces, axis=-1)


def align_pair(low_set, high_set, need_now, fetch_width):
    high_set = widen(high_set, fetch_width)
    low_set = widen(low_set, fetch_width - need_now)
    return (low_set, high_set, fetch_width - need_now)


def delay_of(trial_ids, subband_ids, trial_count, low_share, jitter):
    all_trials = low_share.shape[0] + 1
    rate_rows = jnp.take(low_share, all_trials // trial_count - 1 + subband_ids)
    return (trial_ids * rate_rows + jnp.take(jitter, trial_count - 2 + trial_ids)) // 64


def merge_rows(low_rows, high_rows, shifts, need_now):
    offsets = need_now - shifts
    bit_count = max(need_now.bit_length(), 1)
    moved = high_rows
    for bit_index in range(bit_count):
        step_size = 2**bit_index
        cols = moved.shape[-1]
        selected = (offsets >> bit_index & 1)[:, None] == 1
        moved = jnp.where(selected, moved[:, step_size:], moved[:, : cols - step_size])
    return low_rows + moved


def shards(spectrogram, low_share, jitter):
    trial_dev = spectrogram.shape[0] // SUMMED
    span_time = spectrogram.shape[1]
    all_trials = low_share.shape[0] + 1
    freq_bits = lax.axis_size("freq").bit_length() - 1
    device = lax.axis_index("freq")
    local_counts = []
    trial_count = 2
    while trial_count <= trial_dev:
        local_counts.append(trial_count)
        trial_count = trial_count * 2
    cross_counts = [trial_dev * 2 ** (bit_index + 1) for bit_index in range(freq_bits)]
    need_list = [count_now - 1 for count_now in local_counts + cross_counts] + [
        2 ** (WIDTHS - 1) - 1
    ]
    fetch_plan = []
    for position in range(len(need_list)):
        need_now = need_list[position]
        fetch_plan.append(need_now)
    states = jnp.sum(spectrogram.reshape(trial_dev, SUMMED, span_time), axis=1, dtype=jnp.float32)[
        :, None, :
    ]
    section_index = 0
    for trial_count in local_counts:
        need_now = trial_count - 1
        groups = states.shape[0] // 2
        low_set, high_set, margin = align_pair(
            states[0::2], states[1::2], need_now, fetch_plan[section_index]
        )
        low_rows = jnp.repeat(low_set, 2, axis=1).reshape(groups * trial_count, -1)
        high_rows = jnp.repeat(high_set, 2, axis=1).reshape(groups * trial_count, -1)
        trial_ids = jnp.tile(jnp.arange(trial_count, dtype=jnp.int32), groups)
        subband_ids = device * (trial_dev // trial_count) + jnp.repeat(
            jnp.arange(groups, dtype=jnp.int32), trial_count
        )
        shifts = delay_of(trial_ids, subband_ids, trial_count, low_share, jitter)
        states = merge_rows(low_rows, high_rows, shifts, need_now).reshape(groups, trial_count, -1)
        section_index = section_index + 1
    trial_rows = states[0]
    trial_ids = jnp.arange(trial_dev, dtype=jnp.int32)
    for bit_index in range(freq_bits):
        trial_count = cross_counts[bit_index]
        need_now = trial_count - 1
        partner = swapped(trial_rows, "freq", bit_index)
        upper_half = device >> bit_index & 1
        low_rows = jnp.where(upper_half == 1, partner, trial_rows)
        high_rows = jnp.where(upper_half == 1, trial_rows, partner)
        low_rows, high_rows, margin = align_pair(
            low_rows, high_rows, need_now, fetch_plan[section_index]
        )
        trial_ids = 2 * trial_ids + upper_half
        shifts = delay_of(trial_ids, device >> bit_index + 1, trial_count, low_share, jitter)
        trial_rows = merge_rows(low_rows, high_rows, shifts, need_now)
        section_index = section_index + 1
    trial_rows = widen(trial_rows, fetch_plan[section_index])
    signal = trial_rows / math.sqrt(all_trials * SUMMED)
    peak_rows = []
    window_sum = signal
    width_now = 1
    for level_index in range(WIDTHS):
        length = window_sum.shape[1]
        peak_rows.append(
            jnp.max(window_sum[:, length - span_time :], axis=0) / math.sqrt(width_now)
        )
        if level_index + 1 < WIDTHS:
            window_sum = window_sum[:, width_now:] + window_sum[:, : length - width_now]
            width_now = width_now * 2
    local_best = jnp.stack(peak_rows)
    for bit_index in range(freq_bits):
        local_best = jnp.maximum(local_best, swapped(local_best, "freq", bit_index))
    return local_best


def solution(mesh):
    placed = (P("freq", "tm"), P(), P())
    return jax.shard_map(
        shards, mesh=mesh, in_specs=placed, out_specs=P(None, "tm"), check_vma=False
    )
```

```python
import math

import jax
import jax.numpy as jnp
from jax import lax
from jax.sharding import PartitionSpec as P

SUMMED = 32
WIDTHS = 9


def swapped(block, axis, apart):
    count = lax.axis_size(axis)
    route = []
    for low in range(count):
        high = low | 1 << apart
        if high != low and high < count:
            route += [(low, high), (high, low)]
    return lax.ppermute(block, axis, route)


def delay_of(trial_ids, subband_ids, trial_count, low_share, jitter):
    all_trials = low_share.shape[0] + 1
    rate_rows = jnp.take(low_share, all_trials // trial_count - 1 + subband_ids)
    return (trial_ids * rate_rows + jnp.take(jitter, trial_count - 2 + trial_ids)) // 64


def zero_front(rows, width):
    return jnp.pad(rows, [(0, 0)] * (rows.ndim - 1) + [(width, 0)])


def merge_rows(low_rows, high_rows, shifts, need_now):
    offsets = need_now - shifts
    bit_count = max(need_now.bit_length(), 1)
    moved = high_rows
    for bit_index in range(bit_count):
        step_size = 2**bit_index
        cols = moved.shape[-1]
        selected = (offsets >> bit_index & 1)[:, None] == 1
        moved = jnp.where(selected, moved[:, step_size:], moved[:, : cols - step_size])
    return low_rows + moved


def halved_max(block, axis, apart, keep_bit):
    parts = block.shape[-2] // 2
    split = block.reshape(block.shape[:-2] + (2, parts) + block.shape[-1:])
    kept = jnp.where(keep_bit == 1, split[..., 1, :, :], split[..., 0, :, :])
    given = jnp.where(keep_bit == 1, split[..., 0, :, :], split[..., 1, :, :])
    return jnp.maximum(kept, swapped(given, axis, apart))


def shards(spectrogram, low_share, jitter):
    sub_dev = spectrogram.shape[0] // SUMMED
    span_time = spectrogram.shape[1]
    all_trials = low_share.shape[0] + 1
    freq_bits = lax.axis_size("freq").bit_length() - 1
    tm_count = lax.axis_size("tm")
    tm_bits = tm_count.bit_length() - 1
    device = lax.axis_index("freq")
    place = lax.axis_index("tm")
    base = jnp.sum(spectrogram.reshape(sub_dev, SUMMED, span_time), axis=1, dtype=jnp.float32)
    base = lax.all_gather(base, "tm", axis=1, tiled=True)
    full_time = base.shape[1]
    states = base[:, None, :]
    trial_count = 2
    while trial_count <= sub_dev:
        need_now = trial_count - 1
        groups = states.shape[0] // 2
        low_rows = jnp.repeat(states[0::2], 2, axis=1).reshape(groups * trial_count, -1)
        high_rows = jnp.repeat(zero_front(states[1::2], need_now), 2, axis=1).reshape(
            groups * trial_count, -1
        )
        trial_ids = jnp.tile(jnp.arange(trial_count, dtype=jnp.int32), groups)
        subband_ids = device * (sub_dev // trial_count) + jnp.repeat(
            jnp.arange(groups, dtype=jnp.int32), trial_count
        )
        shifts = delay_of(trial_ids, subband_ids, trial_count, low_share, jitter)
        states = merge_rows(low_rows, high_rows, shifts, need_now).reshape(
            groups, trial_count, -1
        )
        trial_count = trial_count * 2
    held = sub_dev // tm_count
    trial_rows = lax.dynamic_slice_in_dim(states[0], place * held, held, axis=0)
    trial_ids = place * held + jnp.arange(held, dtype=jnp.int32)
    for bit_index in range(freq_bits):
        trial_count = sub_dev * 2 ** (bit_index + 1)
        need_now = trial_count - 1
        partner = swapped(trial_rows, "freq", bit_index)
        upper_half = device >> bit_index & 1
        low_rows = jnp.where(upper_half == 1, partner, trial_rows)
        high_rows = jnp.where(upper_half == 1, trial_rows, partner)
        trial_ids = 2 * trial_ids + upper_half
        shifts = delay_of(trial_ids, device >> bit_index + 1, trial_count, low_share, jitter)
        trial_rows = merge_rows(low_rows, zero_front(high_rows, need_now), shifts, need_now)
    signal = trial_rows / math.sqrt(all_trials * SUMMED)
    peak_rows = []
    window_sum = signal
    width_now = 1
    for level_index in range(WIDTHS):
        peak_rows.append(jnp.max(window_sum, axis=0) / math.sqrt(width_now))
        if level_index + 1 < WIDTHS:
            window_sum = window_sum + zero_front(window_sum, width_now)[:, :full_time]
            width_now = width_now * 2
    best = jnp.stack(peak_rows).reshape(WIDTHS, tm_count, span_time)
    for bit_index in reversed(range(tm_bits)):
        best = halved_max(best, "tm", bit_index, place >> bit_index & 1)
    best = best.reshape(WIDTHS, span_time)
    for bit_index in range(freq_bits):
        best = jnp.maximum(best, swapped(best, "freq", bit_index))
    return best


def solution(mesh):
    placed = (P("freq", "tm"), P(), P())
    return jax.shard_map(
        shards, mesh=mesh, in_specs=placed, out_specs=P(None, "tm"), check_vma=False
    )
```

```python
import math

import jax
import jax.numpy as jnp
from jax import lax
from jax.sharding import PartitionSpec as P

SUMMED = 32
WIDTHS = 9
SHARED_LEVELS = 3


def swapped(block, axis, apart):
    count = lax.axis_size(axis)
    route = []
    for low in range(count):
        high = low | 1 << apart
        if high != low and high < count:
            route += [(low, high), (high, low)]
    return lax.ppermute(block, axis, route)


def zero_front(rows, width):
    return jnp.pad(rows, [(0, 0)] * (rows.ndim - 1) + [(width, 0)])


def merge_rows(low_rows, high_rows, shifts, need_now):
    offsets = need_now - shifts
    bit_count = max(need_now.bit_length(), 1)
    moved = high_rows
    for bit_index in range(bit_count):
        step_size = 2**bit_index
        cols = moved.shape[-1]
        selected = (offsets >> bit_index & 1)[:, None] == 1
        moved = jnp.where(selected, moved[:, step_size:], moved[:, : cols - step_size])
    return low_rows + moved


def shards(spectrogram, low_share, jitter):
    sub_dev = spectrogram.shape[0] // SUMMED
    span_time = spectrogram.shape[1]
    all_trials = low_share.shape[0] + 1
    freq_bits = lax.axis_size("freq").bit_length() - 1
    tm_count = lax.axis_size("tm")
    shared = min(SHARED_LEVELS, freq_bits)
    device = lax.axis_index("freq")
    place = lax.axis_index("tm")
    held = sub_dev // tm_count

    rate_index, jitter_index, level_rows = [], [], []
    trial_count = 2
    while trial_count <= sub_dev:
        groups = sub_dev // trial_count
        trial_ids = jnp.tile(jnp.arange(trial_count, dtype=jnp.int32), groups)
        subband_ids = device * groups + jnp.repeat(jnp.arange(groups, dtype=jnp.int32), trial_count)
        rate_index.append(all_trials // trial_count - 1 + subband_ids)
        jitter_index.append(trial_count - 2 + trial_ids)
        level_rows.append(trial_ids)
        trial_count = trial_count * 2
    trial_ids = place * held + jnp.arange(held, dtype=jnp.int32)
    for bit_index in range(freq_bits):
        trial_count = sub_dev * 2 ** (bit_index + 1)
        if bit_index >= freq_bits - shared:
            trial_ids = (2 * trial_ids[:, None] + jnp.arange(2, dtype=jnp.int32)).reshape(-1)
        else:
            trial_ids = 2 * trial_ids + (device >> bit_index & 1)
        subband_ids = jnp.broadcast_to(device >> bit_index + 1, trial_ids.shape)
        rate_index.append(all_trials // trial_count - 1 + subband_ids)
        jitter_index.append(trial_count - 2 + trial_ids)
        level_rows.append(trial_ids)
    rates = jnp.take(low_share, jnp.concatenate(rate_index))
    jitters = jnp.take(jitter, jnp.concatenate(jitter_index))
    ids_all = jnp.concatenate(level_rows)
    shift_table = (ids_all * rates + jitters) // 64
    level_shifts = []
    start = 0
    for rows in level_rows:
        level_shifts.append(shift_table[start : start + rows.shape[0]])
        start = start + rows.shape[0]

    base = jnp.sum(spectrogram.reshape(sub_dev, SUMMED, span_time), axis=1, dtype=jnp.float32)
    spread = jnp.broadcast_to(base[None], (tm_count,) + base.shape)
    gathered = lax.all_to_all(spread, "tm", 0, 0, tiled=True)
    base = jnp.transpose(gathered, (1, 0, 2)).reshape(sub_dev, tm_count * span_time)
    full_time = base.shape[1]
    states = base[:, None, :]
    level = 0
    trial_count = 2
    while trial_count <= sub_dev:
        need_now = trial_count - 1
        groups = states.shape[0] // 2
        low_rows = jnp.repeat(states[0::2], 2, axis=1).reshape(groups * trial_count, -1)
        high_rows = jnp.repeat(zero_front(states[1::2], need_now), 2, axis=1).reshape(
            groups * trial_count, -1
        )
        states = merge_rows(low_rows, high_rows, level_shifts[level], need_now).reshape(
            groups, trial_count, -1
        )
        level = level + 1
        trial_count = trial_count * 2
    trial_rows = lax.dynamic_slice_in_dim(states[0], place * held, held, axis=0)
    for bit_index in range(freq_bits):
        need_now = sub_dev * 2 ** (bit_index + 1) - 1
        partner = swapped(trial_rows, "freq", bit_index)
        upper_half = device >> bit_index & 1
        low_rows = jnp.where(upper_half == 1, partner, trial_rows)
        high_rows = jnp.where(upper_half == 1, trial_rows, partner)
        if bit_index >= freq_bits - shared:
            low_rows = jnp.repeat(low_rows, 2, axis=0)
            high_rows = jnp.repeat(high_rows, 2, axis=0)
        trial_rows = merge_rows(
            low_rows, zero_front(high_rows, need_now), level_shifts[level], need_now
        )
        level = level + 1
    signal = trial_rows / math.sqrt(all_trials * SUMMED)
    peak_rows = []
    window_sum = signal
    width_now = 1
    for level_index in range(WIDTHS):
        peak_rows.append(jnp.max(window_sum, axis=0) / math.sqrt(width_now))
        if level_index + 1 < WIDTHS:
            window_sum = window_sum + zero_front(window_sum, width_now)[:, :full_time]
            width_now = width_now * 2
    best = jnp.stack(peak_rows).reshape(WIDTHS, tm_count, span_time)
    best = jnp.max(lax.all_to_all(best, "tm", 1, 1, tiled=True), axis=1)
    for bit_index in range(freq_bits - shared):
        best = jnp.maximum(best, swapped(best, "freq", bit_index))
    return best


def solution(mesh):
    placed = (P("freq", "tm"), P(), P())
    return jax.shard_map(
        shards, mesh=mesh, in_specs=placed, out_specs=P(None, "tm"), check_vma=False
    )
```

```python
import math

import numpy as np
import jax
import jax.numpy as jnp
from jax import lax
from jax.sharding import PartitionSpec as P

SUMMED = 32
WIDTHS = 9
SHARED_LEVELS = 3
NEAR_HALF = (6, 7, 4, 5, 2, 3, 0, 1)


def swapped(block, axis, apart):
    count = lax.axis_size(axis)
    route = []
    for low in range(count):
        high = low | 1 << apart
        if high != low and high < count:
            route += [(low, high), (high, low)]
    return lax.ppermute(block, axis, route)


def paired(block, axis, partner_of):
    return lax.ppermute(block, axis, [(partner_of(i), i) for i in range(lax.axis_size(axis))])


def near_half(bit_index, ring_bits):
    def partner_of(i):
        ring = i >> ring_bits & 7
        return i - (ring << ring_bits) + (NEAR_HALF[ring] << ring_bits)

    return partner_of


def zero_front(rows, width):
    return jnp.pad(rows, [(0, 0)] * (rows.ndim - 1) + [(width, 0)])


def merge_rows(low_rows, high_rows, shifts, need_now):
    offsets = need_now - shifts
    bit_count = max(need_now.bit_length(), 1)
    moved = high_rows
    for bit_index in range(bit_count):
        step_size = 2**bit_index
        cols = moved.shape[-1]
        selected = (offsets >> bit_index & 1)[:, None] == 1
        moved = jnp.where(selected, moved[:, step_size:], moved[:, : cols - step_size])
    return low_rows + moved


def delay_plan(sub_dev, held, freq_bits, shared, all_trials):
    terms = 2 + freq_bits
    ids, rates, jits, level_rows = [], [], [], []
    trial_count = 2
    while trial_count <= sub_dev:
        groups = sub_dev // trial_count
        rows = groups * trial_count
        trial = np.tile(np.arange(trial_count), groups)
        group = np.repeat(np.arange(groups), trial_count)
        one_id = np.zeros((terms, rows), np.int64)
        one_id[0] = trial
        one_rate = np.zeros((terms, rows), np.int64)
        one_rate[0] = all_trials // trial_count - 1 + group
        for bit in range(freq_bits):
            one_rate[2 + bit] = groups << bit
        ids.append(one_id)
        rates.append(one_rate)
        level_rows.append(rows)
        trial_count = trial_count * 2
    now = np.zeros((terms, held), np.int64)
    now[0] = np.arange(held)
    now[1] = held
    for bit_index in range(freq_bits):
        trial_count = sub_dev * 2 ** (bit_index + 1)
        if bit_index >= freq_bits - shared:
            now = 2 * np.repeat(now, 2, axis=1)
            now[0] = now[0] + np.tile(np.arange(2), now.shape[1] // 2)
        else:
            now = 2 * now
            now[2 + bit_index] = now[2 + bit_index] + 1
        one_rate = np.zeros_like(now)
        one_rate[0] = all_trials // trial_count - 1
        for bit in range(bit_index + 1, freq_bits):
            one_rate[2 + bit] = 1 << (bit - bit_index - 1)
        ids.append(now.copy())
        rates.append(one_rate)
        level_rows.append(now.shape[1])
    counts = []
    trial_count = 2
    while trial_count <= sub_dev:
        counts.append(trial_count)
        trial_count = trial_count * 2
    counts += [sub_dev * 2 ** (bit_index + 1) for bit_index in range(freq_bits)]
    jit_rows = [one_id.copy() for one_id in ids]
    for one_jit, trial_count in zip(jit_rows, counts):
        one_jit[0] = one_jit[0] + trial_count - 2
    pack = lambda parts: np.concatenate(parts, axis=1).astype(np.int32)
    return pack(ids), pack(rates), pack(jit_rows), level_rows


def shards(spectrogram, low_share, jitter):
    sub_dev = spectrogram.shape[0] // SUMMED
    span_time = spectrogram.shape[1]
    all_trials = low_share.shape[0] + 1
    freq_bits = lax.axis_size("freq").bit_length() - 1
    tm_count = lax.axis_size("tm")
    shared = min(SHARED_LEVELS, freq_bits)
    device = lax.axis_index("freq")
    place = lax.axis_index("tm")
    held = sub_dev // tm_count

    id_terms, rate_terms, jitter_terms, level_rows = delay_plan(
        sub_dev, held, freq_bits, shared, all_trials
    )
    factors = jnp.concatenate(
        [jnp.ones((1,), jnp.int32), place[None].astype(jnp.int32),
         (device >> jnp.arange(freq_bits, dtype=jnp.int32) & 1).astype(jnp.int32)]
    )[:, None]
    ids_all = jnp.sum(factors * id_terms, axis=0)
    rates = jnp.take(low_share, jnp.sum(factors * rate_terms, axis=0))
    jitters = jnp.take(jitter, jnp.sum(factors * jitter_terms, axis=0))
    shift_table = (ids_all * rates + jitters) // 64
    level_shifts = []
    start = 0
    for rows in level_rows:
        level_shifts.append(shift_table[start : start + rows])
        start = start + rows

    base = jnp.sum(spectrogram.reshape(sub_dev, SUMMED, span_time), axis=1, dtype=jnp.float32)
    spread = jnp.broadcast_to(base[None], (tm_count,) + base.shape)
    gathered = lax.all_to_all(spread, "tm", 0, 0, tiled=True)
    base = jnp.transpose(gathered, (1, 0, 2)).reshape(sub_dev, tm_count * span_time)
    full_time = base.shape[1]
    states = base[:, None, :]
    level = 0
    trial_count = 2
    while trial_count <= sub_dev:
        need_now = trial_count - 1
        groups = states.shape[0] // 2
        low_rows = jnp.repeat(states[0::2], 2, axis=1).reshape(groups * trial_count, -1)
        high_rows = jnp.repeat(zero_front(states[1::2], need_now), 2, axis=1).reshape(
            groups * trial_count, -1
        )
        states = merge_rows(low_rows, high_rows, level_shifts[level], need_now).reshape(
            groups, trial_count, -1
        )
        level = level + 1
        trial_count = trial_count * 2
    trial_rows = lax.dynamic_slice_in_dim(states[0], place * held, held, axis=0)
    for bit_index in range(freq_bits):
        need_now = sub_dev * 2 ** (bit_index + 1) - 1
        if bit_index == freq_bits - 1 and shared >= 3 and bit_index >= 2:
            partner = paired(trial_rows, "freq", near_half(bit_index, bit_index - 2))
        else:
            partner = swapped(trial_rows, "freq", bit_index)
        upper_half = device >> bit_index & 1
        low_rows = jnp.where(upper_half == 1, partner, trial_rows)
        high_rows = jnp.where(upper_half == 1, trial_rows, partner)
        if bit_index >= freq_bits - shared:
            low_rows = jnp.repeat(low_rows, 2, axis=0)
            high_rows = jnp.repeat(high_rows, 2, axis=0)
        trial_rows = merge_rows(
            low_rows, zero_front(high_rows, need_now), level_shifts[level], need_now
        )
        level = level + 1
    signal = trial_rows / math.sqrt(all_trials * SUMMED)
    peak_rows = []
    window_sum = signal
    width_now = 1
    for level_index in range(WIDTHS):
        peak_rows.append(jnp.max(window_sum, axis=0) / math.sqrt(width_now))
        if level_index + 1 < WIDTHS:
            window_sum = window_sum + zero_front(window_sum, width_now)[:, :full_time]
            width_now = width_now * 2
    best = jnp.stack(peak_rows).reshape(WIDTHS, tm_count, span_time)
    best = jnp.max(lax.all_to_all(best, "tm", 1, 1, tiled=True), axis=1)
    for bit_index in range(freq_bits - shared):
        if bit_index == 3:
            best = jnp.maximum(best, paired(best, "freq", near_half(bit_index, 1)))
        else:
            best = jnp.maximum(best, swapped(best, "freq", bit_index))
    return best


def solution(mesh):
    placed = (P("freq", "tm"), P(), P())
    return jax.shard_map(
        shards, mesh=mesh, in_specs=placed, out_specs=P(None, "tm"), check_vma=False
    )
```

```python
import functools
import math

import numpy as np
import jax
import jax.numpy as jnp
from jax import lax
from jax.experimental import pallas as pl
from jax.experimental.pallas import tpu as pltpu
from jax.sharding import PartitionSpec as P

SUMMED = 32
WIDTHS = 9
SHARED_LEVELS = 3
NEAR_HALF = (6, 7, 4, 5, 2, 3, 0, 1)


def swapped(block, axis, apart):
    count = lax.axis_size(axis)
    route = []
    for low in range(count):
        high = low | 1 << apart
        if high != low and high < count:
            route += [(low, high), (high, low)]
    return lax.ppermute(block, axis, route)


def paired(block, axis, partner_of):
    return lax.ppermute(block, axis, [(partner_of(i), i) for i in range(lax.axis_size(axis))])


def near_half(bit_index, ring_bits):
    def partner_of(i):
        ring = i >> ring_bits & 7
        return i - (ring << ring_bits) + (NEAR_HALF[ring] << ring_bits)

    return partner_of


def zero_front(rows, width):
    return jnp.pad(rows, [(0, 0)] * (rows.ndim - 1) + [(width, 0)])


def merge_kernel(bit_count, shift_ref, low_ref, high_ref, out_ref):
    shifts = shift_ref[...]
    moved = high_ref[...]
    for bit_index in range(bit_count):
        rolled = pltpu.roll(moved, 1 << bit_index, 1)
        moved = jnp.where((shifts >> bit_index & 1) == 1, rolled, moved)
    col = lax.broadcasted_iota(jnp.int32, moved.shape, 1)
    out_ref[...] = low_ref[...] + jnp.where(col >= shifts, moved, 0.0)


def merge_rows(low_rows, high_rows, shifts, need_now):
    rows, cols = low_rows.shape
    return pl.pallas_call(
        functools.partial(merge_kernel, max(need_now.bit_length(), 1)),
        out_shape=jax.ShapeDtypeStruct((rows, cols), jnp.float32),
        cost_estimate=pl.CostEstimate(
            flops=rows * cols * 24, transcendentals=0, bytes_accessed=rows * cols * 12
        ),
    )(shifts[:, None].astype(jnp.int32), low_rows, high_rows)


def delay_plan(sub_dev, held, freq_bits, shared, all_trials):
    terms = 2 + freq_bits
    ids, rates, jits, level_rows = [], [], [], []
    trial_count = 2
    while trial_count <= sub_dev:
        groups = sub_dev // trial_count
        rows = groups * trial_count
        trial = np.tile(np.arange(trial_count), groups)
        group = np.repeat(np.arange(groups), trial_count)
        one_id = np.zeros((terms, rows), np.int64)
        one_id[0] = trial
        one_rate = np.zeros((terms, rows), np.int64)
        one_rate[0] = all_trials // trial_count - 1 + group
        for bit in range(freq_bits):
            one_rate[2 + bit] = groups << bit
        ids.append(one_id)
        rates.append(one_rate)
        level_rows.append(rows)
        trial_count = trial_count * 2
    now = np.zeros((terms, held), np.int64)
    now[0] = np.arange(held)
    now[1] = held
    for bit_index in range(freq_bits):
        trial_count = sub_dev * 2 ** (bit_index + 1)
        if bit_index >= freq_bits - shared:
            now = 2 * np.repeat(now, 2, axis=1)
            now[0] = now[0] + np.tile(np.arange(2), now.shape[1] // 2)
        else:
            now = 2 * now
            now[2 + bit_index] = now[2 + bit_index] + 1
        one_rate = np.zeros_like(now)
        one_rate[0] = all_trials // trial_count - 1
        for bit in range(bit_index + 1, freq_bits):
            one_rate[2 + bit] = 1 << (bit - bit_index - 1)
        ids.append(now.copy())
        rates.append(one_rate)
        level_rows.append(now.shape[1])
    counts = []
    trial_count = 2
    while trial_count <= sub_dev:
        counts.append(trial_count)
        trial_count = trial_count * 2
    counts += [sub_dev * 2 ** (bit_index + 1) for bit_index in range(freq_bits)]
    jit_rows = [one_id.copy() for one_id in ids]
    for one_jit, trial_count in zip(jit_rows, counts):
        one_jit[0] = one_jit[0] + trial_count - 2
    pack = lambda parts: np.concatenate(parts, axis=1).astype(np.int32)
    return pack(ids), pack(rates), pack(jit_rows), level_rows


def shards(spectrogram, low_share, jitter):
    sub_dev = spectrogram.shape[0] // SUMMED
    span_time = spectrogram.shape[1]
    all_trials = low_share.shape[0] + 1
    freq_bits = lax.axis_size("freq").bit_length() - 1
    tm_count = lax.axis_size("tm")
    shared = min(SHARED_LEVELS, freq_bits)
    device = lax.axis_index("freq")
    place = lax.axis_index("tm")
    held = sub_dev // tm_count

    id_terms, rate_terms, jitter_terms, level_rows = delay_plan(
        sub_dev, held, freq_bits, shared, all_trials
    )
    factors = jnp.concatenate(
        [jnp.ones((1,), jnp.int32), place[None].astype(jnp.int32),
         (device >> jnp.arange(freq_bits, dtype=jnp.int32) & 1).astype(jnp.int32)]
    )[:, None]
    ids_all = jnp.sum(factors * id_terms, axis=0)
    rates = jnp.take(low_share, jnp.sum(factors * rate_terms, axis=0))
    jitters = jnp.take(jitter, jnp.sum(factors * jitter_terms, axis=0))
    shift_table = (ids_all * rates + jitters) // 64
    level_shifts = []
    start = 0
    for rows in level_rows:
        level_shifts.append(shift_table[start : start + rows])
        start = start + rows

    base = jnp.sum(spectrogram.reshape(sub_dev, SUMMED, span_time), axis=1, dtype=jnp.float32)
    spread = jnp.broadcast_to(base[None], (tm_count,) + base.shape)
    gathered = lax.all_to_all(spread, "tm", 0, 0, tiled=True)
    base = jnp.transpose(gathered, (1, 0, 2)).reshape(sub_dev, tm_count * span_time)
    full_time = base.shape[1]
    states = base[:, None, :]
    level = 0
    trial_count = 2
    while trial_count <= sub_dev:
        need_now = trial_count - 1
        groups = states.shape[0] // 2
        low_rows = jnp.repeat(states[0::2], 2, axis=1).reshape(groups * trial_count, -1)
        high_rows = jnp.repeat(states[1::2], 2, axis=1).reshape(
            groups * trial_count, -1
        )
        states = merge_rows(low_rows, high_rows, level_shifts[level], need_now).reshape(
            groups, trial_count, -1
        )
        level = level + 1
        trial_count = trial_count * 2
    trial_rows = lax.dynamic_slice_in_dim(states[0], place * held, held, axis=0)
    for bit_index in range(freq_bits):
        need_now = sub_dev * 2 ** (bit_index + 1) - 1
        if bit_index == freq_bits - 1 and shared >= 3 and bit_index >= 2:
            partner = paired(trial_rows, "freq", near_half(bit_index, bit_index - 2))
        else:
            partner = swapped(trial_rows, "freq", bit_index)
        upper_half = device >> bit_index & 1
        low_rows = jnp.where(upper_half == 1, partner, trial_rows)
        high_rows = jnp.where(upper_half == 1, trial_rows, partner)
        if bit_index >= freq_bits - shared:
            low_rows = jnp.repeat(low_rows, 2, axis=0)
            high_rows = jnp.repeat(high_rows, 2, axis=0)
        trial_rows = merge_rows(low_rows, high_rows, level_shifts[level], need_now)
        level = level + 1
    signal = trial_rows / math.sqrt(all_trials * SUMMED)
    peak_rows = []
    window_sum = signal
    width_now = 1
    for level_index in range(WIDTHS):
        peak_rows.append(jnp.max(window_sum, axis=0) / math.sqrt(width_now))
        if level_index + 1 < WIDTHS:
            window_sum = window_sum + zero_front(window_sum, width_now)[:, :full_time]
            width_now = width_now * 2
    best = jnp.stack(peak_rows).reshape(WIDTHS, tm_count, span_time)
    best = jnp.max(lax.all_to_all(best, "tm", 1, 1, tiled=True), axis=1)
    for bit_index in range(freq_bits - shared):
        if bit_index == 3:
            best = jnp.maximum(best, paired(best, "freq", near_half(bit_index, 1)))
        else:
            best = jnp.maximum(best, swapped(best, "freq", bit_index))
    return best


def solution(mesh):
    placed = (P("freq", "tm"), P(), P())
    return jax.shard_map(
        shards, mesh=mesh, in_specs=placed, out_specs=P(None, "tm"), check_vma=False
    )
```

```python
import math

import numpy as np
import jax
import jax.numpy as jnp
from jax import lax
from jax.sharding import PartitionSpec as P

SUMMED = 32
WIDTHS = 9
SHARED_LEVELS = 4
NEAR_HALF = (6, 7, 4, 5, 2, 3, 0, 1)
NEXT_PAIR = (7, 2, 1, 4, 3, 6, 5, 0)


def swapped(block, axis, apart):
    count = lax.axis_size(axis)
    route = []
    for low in range(count):
        high = low | 1 << apart
        if high != low and high < count:
            route += [(low, high), (high, low)]
    return lax.ppermute(block, axis, route)


def paired(block, axis, partner_of):
    return lax.ppermute(block, axis, [(partner_of(i), i) for i in range(lax.axis_size(axis))])


def ring_partner(table, ring_bits):
    def partner_of(i):
        ring = i >> ring_bits & 7
        return i - (ring << ring_bits) + (table[ring] << ring_bits)

    return partner_of


def zero_front(rows, width):
    return jnp.pad(rows, [(0, 0)] * (rows.ndim - 1) + [(width, 0)])


def merge_rows(low_rows, high_rows, shifts, need_now):
    offsets = need_now - shifts
    bit_count = max(need_now.bit_length(), 1)
    moved = high_rows
    for bit_index in range(bit_count):
        step_size = 2**bit_index
        cols = moved.shape[-1]
        selected = (offsets >> bit_index & 1)[:, None] == 1
        moved = jnp.where(selected, moved[:, step_size:], moved[:, : cols - step_size])
    return low_rows + moved


def delay_plan(sub_dev, held, freq_bits, shared, all_trials):
    terms = 2 + freq_bits
    ids, rates, jits, level_rows = [], [], [], []
    trial_count = 2
    while trial_count <= sub_dev:
        groups = sub_dev // trial_count
        rows = groups * trial_count
        trial = np.tile(np.arange(trial_count), groups)
        group = np.repeat(np.arange(groups), trial_count)
        one_id = np.zeros((terms, rows), np.int64)
        one_id[0] = trial
        one_rate = np.zeros((terms, rows), np.int64)
        one_rate[0] = all_trials // trial_count - 1 + group
        for bit in range(freq_bits):
            one_rate[2 + bit] = groups << bit
        ids.append(one_id)
        rates.append(one_rate)
        level_rows.append(rows)
        trial_count = trial_count * 2
    now = np.zeros((terms, held), np.int64)
    now[0] = np.arange(held)
    now[1] = held
    for bit_index in range(freq_bits):
        trial_count = sub_dev * 2 ** (bit_index + 1)
        if bit_index >= freq_bits - shared:
            now = 2 * np.repeat(now, 2, axis=1)
            now[0] = now[0] + np.tile(np.arange(2), now.shape[1] // 2)
        else:
            now = 2 * now
            now[2 + bit_index] = now[2 + bit_index] + 1
        one_rate = np.zeros_like(now)
        one_rate[0] = all_trials // trial_count - 1
        for bit in range(bit_index + 1, freq_bits):
            one_rate[2 + bit] = 1 << (bit - bit_index - 1)
        ids.append(now.copy())
        rates.append(one_rate)
        level_rows.append(now.shape[1])
    counts = []
    trial_count = 2
    while trial_count <= sub_dev:
        counts.append(trial_count)
        trial_count = trial_count * 2
    counts += [sub_dev * 2 ** (bit_index + 1) for bit_index in range(freq_bits)]
    jit_rows = [one_id.copy() for one_id in ids]
    for one_jit, trial_count in zip(jit_rows, counts):
        one_jit[0] = one_jit[0] + trial_count - 2
    pack = lambda parts: np.concatenate(parts, axis=1).astype(np.int32)
    return pack(ids), pack(rates), pack(jit_rows), level_rows


def shards(spectrogram, low_share, jitter):
    sub_dev = spectrogram.shape[0] // SUMMED
    span_time = spectrogram.shape[1]
    all_trials = low_share.shape[0] + 1
    freq_bits = lax.axis_size("freq").bit_length() - 1
    tm_count = lax.axis_size("tm")
    shared = min(SHARED_LEVELS, freq_bits)
    device = lax.axis_index("freq")
    place = lax.axis_index("tm")
    held = sub_dev // tm_count

    id_terms, rate_terms, jitter_terms, level_rows = delay_plan(
        sub_dev, held, freq_bits, shared, all_trials
    )
    factors = jnp.concatenate(
        [jnp.ones((1,), jnp.int32), place[None].astype(jnp.int32),
         (device >> jnp.arange(freq_bits, dtype=jnp.int32) & 1).astype(jnp.int32)]
    )[:, None]
    ids_all = jnp.sum(factors * id_terms, axis=0)
    rates = jnp.take(low_share, jnp.sum(factors * rate_terms, axis=0))
    jitters = jnp.take(jitter, jnp.sum(factors * jitter_terms, axis=0))
    shift_table = (ids_all * rates + jitters) // 64
    level_shifts = []
    start = 0
    for rows in level_rows:
        level_shifts.append(shift_table[start : start + rows])
        start = start + rows

    base = jnp.sum(spectrogram.reshape(sub_dev, SUMMED, span_time), axis=1, dtype=jnp.float32)
    spread = jnp.broadcast_to(base[None], (tm_count,) + base.shape)
    gathered = lax.all_to_all(spread, "tm", 0, 0, tiled=True)
    base = jnp.transpose(gathered, (1, 0, 2)).reshape(sub_dev, tm_count * span_time)
    full_time = base.shape[1]
    states = base[:, None, :]
    level = 0
    trial_count = 2
    while trial_count <= sub_dev:
        need_now = trial_count - 1
        groups = states.shape[0] // 2
        low_rows = jnp.repeat(states[0::2], 2, axis=1).reshape(groups * trial_count, -1)
        high_rows = jnp.repeat(zero_front(states[1::2], need_now), 2, axis=1).reshape(
            groups * trial_count, -1
        )
        states = merge_rows(low_rows, high_rows, level_shifts[level], need_now).reshape(
            groups, trial_count, -1
        )
        level = level + 1
        trial_count = trial_count * 2
    trial_rows = lax.dynamic_slice_in_dim(states[0], place * held, held, axis=0)
    for bit_index in range(freq_bits):
        need_now = sub_dev * 2 ** (bit_index + 1) - 1
        if bit_index == freq_bits - 1 and shared >= 3 and bit_index >= 2:
            partner = paired(trial_rows, "freq", ring_partner(NEAR_HALF, bit_index - 2))
        else:
            partner = swapped(trial_rows, "freq", bit_index)
        upper_half = device >> bit_index & 1
        low_rows = jnp.where(upper_half == 1, partner, trial_rows)
        high_rows = jnp.where(upper_half == 1, trial_rows, partner)
        if bit_index >= freq_bits - shared:
            low_rows = jnp.repeat(low_rows, 2, axis=0)
            high_rows = jnp.repeat(high_rows, 2, axis=0)
        trial_rows = merge_rows(
            low_rows, zero_front(high_rows, need_now), level_shifts[level], need_now
        )
        level = level + 1
    signal = trial_rows / math.sqrt(all_trials * SUMMED)
    peak_rows = []
    window_sum = signal
    width_now = 1
    for level_index in range(WIDTHS):
        peak_rows.append(jnp.max(window_sum, axis=0) / math.sqrt(width_now))
        if level_index + 1 < WIDTHS:
            window_sum = window_sum + zero_front(window_sum, width_now)[:, :full_time]
            width_now = width_now * 2
    best = jnp.stack(peak_rows).reshape(WIDTHS, tm_count, span_time)
    best = jnp.max(lax.all_to_all(best, "tm", 1, 1, tiled=True), axis=1)
    for bit_index in range(freq_bits - shared):
        if bit_index == 3:
            best = jnp.maximum(best, paired(best, "freq", ring_partner(NEAR_HALF, 1)))
        elif bit_index == 2 and freq_bits - shared == 3:
            best = jnp.maximum(best, paired(best, "freq", ring_partner(NEXT_PAIR, 1)))
        else:
            best = jnp.maximum(best, swapped(best, "freq", bit_index))
    return best


def solution(mesh):
    placed = (P("freq", "tm"), P(), P())
    return jax.shard_map(
        shards, mesh=mesh, in_specs=placed, out_specs=P(None, "tm"), check_vma=False
    )
```

```python
import math

import numpy as np
import jax
import jax.numpy as jnp
from jax import lax
from jax.sharding import PartitionSpec as P

SUMMED = 32
WIDTHS = 9
SHARED_LEVELS = 3
NEAR_HALF = (6, 7, 4, 5, 2, 3, 0, 1)


def swapped(block, axis, apart):
    count = lax.axis_size(axis)
    route = []
    for low in range(count):
        high = low | 1 << apart
        if high != low and high < count:
            route += [(low, high), (high, low)]
    return lax.ppermute(block, axis, route)


def paired(block, axis, partner_of):
    return lax.ppermute(block, axis, [(partner_of(i), i) for i in range(lax.axis_size(axis))])


def near_half(bit_index, ring_bits):
    def partner_of(i):
        ring = i >> ring_bits & 7
        return i - (ring << ring_bits) + (NEAR_HALF[ring] << ring_bits)

    return partner_of


def zero_front(rows, width):
    return jnp.pad(rows, [(0, 0)] * (rows.ndim - 1) + [(width, 0)])


def merge_rows(low_rows, high_rows, shifts, need_now):
    offsets = need_now - shifts
    bit_count = max(need_now.bit_length(), 1)
    moved = high_rows
    for bit_index in range(bit_count):
        step_size = 2**bit_index
        cols = moved.shape[-1]
        selected = (offsets >> bit_index & 1)[:, None] == 1
        moved = jnp.where(selected, moved[:, step_size:], moved[:, : cols - step_size])
    return low_rows + moved


def shift_rows(rows, shifts, bit_count):
    limit = 2**bit_count - 1
    offsets = limit - shifts
    moved = zero_front(rows, limit)
    for bit_index in range(bit_count):
        step_size = 2**bit_index
        cols = moved.shape[-1]
        selected = (offsets >> bit_index & 1)[:, None] == 1
        moved = jnp.where(selected, moved[:, step_size:], moved[:, : cols - step_size])
    return moved


def delay_plan(sub_dev, held, tm_bits, freq_bits, shared, all_trials):
    terms = 1 + tm_bits + freq_bits
    local_bits = sub_dev.bit_length() - 1
    held_bits = held.bit_length() - 1

    def held_trial(m, right):
        value = np.zeros(terms, np.int64)
        for p in range(held_bits + tm_bits):
            if p < right:
                continue
            if p < held_bits:
                value[0] += (m >> p & 1) << (p - right)
            else:
                value[1 + p - held_bits] += 1 << (p - right)
        return value

    ids, rates, jits = [], [], []
    slot = {}
    for k in range(1, local_bits + 1):
        trial_count = 2**k
        for m in range(held):
            trial = held_trial(m, local_bits - k)
            for g in range(sub_dev >> k):
                key = (k, g, tuple(trial))
                if key in slot:
                    continue
                slot[key] = len(ids)
                rate = np.zeros(terms, np.int64)
                rate[0] = all_trials // trial_count - 1 + g
                for bit in range(freq_bits):
                    rate[1 + tm_bits + bit] = (sub_dev >> k) << bit
                jit = trial.copy()
                jit[0] += trial_count - 2
                ids.append(trial)
                rates.append(rate)
                jits.append(jit)
    paths = np.zeros((held * sub_dev, len(ids)), np.float32)
    for m in range(held):
        for i in range(sub_dev):
            for k in range(1, local_bits + 1):
                if i >> (k - 1) & 1:
                    key = (k, i >> k, tuple(held_trial(m, local_bits - k)))
                    paths[m * sub_dev + i, slot[key]] += 1.0
    unique_count = len(ids)
    level_rows = []
    now = np.zeros((held, terms), np.int64)
    for m in range(held):
        now[m] = held_trial(m, 0)
    for bit_index in range(freq_bits):
        trial_count = sub_dev * 2 ** (bit_index + 1)
        if bit_index >= freq_bits - shared:
            now = 2 * np.repeat(now, 2, axis=0)
            now[:, 0] = now[:, 0] + np.tile(np.arange(2), now.shape[0] // 2)
        else:
            now = 2 * now
            now[:, 1 + tm_bits + bit_index] = now[:, 1 + tm_bits + bit_index] + 1
        rate = np.zeros(terms, np.int64)
        rate[0] = all_trials // trial_count - 1
        for bit in range(bit_index + 1, freq_bits):
            rate[1 + tm_bits + bit] = 1 << (bit - bit_index - 1)
        for row in now:
            jit = row.copy()
            jit[0] += trial_count - 2
            ids.append(row.copy())
            rates.append(rate)
            jits.append(jit)
        level_rows.append(now.shape[0])
    pack = lambda parts: np.stack(parts, axis=1).astype(np.int32)
    return pack(ids), pack(rates), pack(jits), paths, unique_count, level_rows


def shards(spectrogram, low_share, jitter):
    sub_dev = spectrogram.shape[0] // SUMMED
    span_time = spectrogram.shape[1]
    all_trials = low_share.shape[0] + 1
    freq_bits = lax.axis_size("freq").bit_length() - 1
    tm_count = lax.axis_size("tm")
    shared = min(SHARED_LEVELS, freq_bits)
    device = lax.axis_index("freq")
    place = lax.axis_index("tm")
    held = sub_dev // tm_count

    tm_bits = tm_count.bit_length() - 1
    id_terms, rate_terms, jitter_terms, paths, unique_count, level_rows = delay_plan(
        sub_dev, held, tm_bits, freq_bits, shared, all_trials
    )
    factors = jnp.concatenate(
        [jnp.ones((1,), jnp.int32),
         (place >> jnp.arange(tm_bits, dtype=jnp.int32) & 1).astype(jnp.int32),
         (device >> jnp.arange(freq_bits, dtype=jnp.int32) & 1).astype(jnp.int32)]
    )[:, None]
    ids_all = jnp.sum(factors * id_terms, axis=0)
    rates = jnp.take(low_share, jnp.sum(factors * rate_terms, axis=0))
    jitters = jnp.take(jitter, jnp.sum(factors * jitter_terms, axis=0))
    shift_table = (ids_all * rates + jitters) // 64
    path_shift = jnp.dot(
        paths, shift_table[:unique_count].astype(jnp.float32), precision=lax.Precision.HIGHEST
    )
    path_shift = jnp.round(path_shift).astype(jnp.int32)
    level_shifts = []
    start = unique_count
    for rows in level_rows:
        level_shifts.append(shift_table[start : start + rows])
        start = start + rows

    base = jnp.sum(spectrogram.reshape(sub_dev, SUMMED, span_time), axis=1, dtype=jnp.float32)
    spread = jnp.broadcast_to(base[None], (tm_count,) + base.shape)
    gathered = lax.all_to_all(spread, "tm", 0, 0, tiled=True)
    base = jnp.transpose(gathered, (1, 0, 2)).reshape(sub_dev, tm_count * span_time)
    full_time = base.shape[1]
    local_limit = sum(2**k - 1 for k in range(1, sub_dev.bit_length()))
    moved = shift_rows(jnp.tile(base, (held, 1)), path_shift, max(local_limit.bit_length(), 1))
    trial_rows = jnp.sum(moved.reshape(held, sub_dev, full_time), axis=1)
    level = 0
    for bit_index in range(freq_bits):
        need_now = sub_dev * 2 ** (bit_index + 1) - 1
        if bit_index == freq_bits - 1 and shared >= 3 and bit_index >= 2:
            partner = paired(trial_rows, "freq", near_half(bit_index, bit_index - 2))
        else:
            partner = swapped(trial_rows, "freq", bit_index)
        upper_half = device >> bit_index & 1
        low_rows = jnp.where(upper_half == 1, partner, trial_rows)
        high_rows = jnp.where(upper_half == 1, trial_rows, partner)
        if bit_index >= freq_bits - shared:
            low_rows = jnp.repeat(low_rows, 2, axis=0)
            high_rows = jnp.repeat(high_rows, 2, axis=0)
        trial_rows = merge_rows(
            low_rows, zero_front(high_rows, need_now), level_shifts[level], need_now
        )
        level = level + 1
    signal = trial_rows / math.sqrt(all_trials * SUMMED)
    peak_rows = []
    window_sum = signal
    width_now = 1
    for level_index in range(WIDTHS):
        peak_rows.append(jnp.max(window_sum, axis=0) / math.sqrt(width_now))
        if level_index + 1 < WIDTHS:
            window_sum = window_sum + zero_front(window_sum, width_now)[:, :full_time]
            width_now = width_now * 2
    best = jnp.stack(peak_rows).reshape(WIDTHS, tm_count, span_time)
    best = jnp.max(lax.all_to_all(best, "tm", 1, 1, tiled=True), axis=1)
    for bit_index in range(freq_bits - shared):
        if bit_index == 3:
            best = jnp.maximum(best, paired(best, "freq", near_half(bit_index, 1)))
        else:
            best = jnp.maximum(best, swapped(best, "freq", bit_index))
    return best


def solution(mesh):
    placed = (P("freq", "tm"), P(), P())
    return jax.shard_map(
        shards, mesh=mesh, in_specs=placed, out_specs=P(None, "tm"), check_vma=False
    )
```

```python
import math

import numpy as np
import jax
import jax.numpy as jnp
from jax import lax
from jax.sharding import PartitionSpec as P

SUMMED = 32
WIDTHS = 9
SHARED_LEVELS = 3
NEAR_HALF = (6, 7, 4, 5, 2, 3, 0, 1)


def swapped(block, axis, apart):
    count = lax.axis_size(axis)
    route = []
    for low in range(count):
        high = low | 1 << apart
        if high != low and high < count:
            route += [(low, high), (high, low)]
    return lax.ppermute(block, axis, route)


def paired(block, axis, partner_of):
    return lax.ppermute(block, axis, [(partner_of(i), i) for i in range(lax.axis_size(axis))])


def near_half(bit_index, ring_bits):
    def partner_of(i):
        ring = i >> ring_bits & 7
        return i - (ring << ring_bits) + (NEAR_HALF[ring] << ring_bits)

    return partner_of


def zero_front(rows, width):
    return jnp.pad(rows, [(0, 0)] * (rows.ndim - 1) + [(width, 0)])


def merge_rows(low_rows, high_rows, shifts, need_now):
    offsets = need_now - shifts
    bit_count = max(need_now.bit_length(), 1)
    moved = high_rows
    for bit_index in range(bit_count):
        step_size = 2**bit_index
        cols = moved.shape[-1]
        selected = (offsets >> bit_index & 1)[:, None] == 1
        moved = jnp.where(selected, moved[:, step_size:], moved[:, : cols - step_size])
    return low_rows + moved


def shift_rows(rows, shifts, bit_count):
    limit = 2**bit_count - 1
    offsets = limit - shifts
    moved = zero_front(rows, limit)
    for bit_index in range(bit_count):
        step_size = 2**bit_index
        cols = moved.shape[-1]
        selected = (offsets >> bit_index & 1)[:, None] == 1
        moved = jnp.where(selected, moved[:, step_size:], moved[:, : cols - step_size])
    return moved


def picked(table, index):
    hit = index[:, None] == jnp.arange(table.shape[0], dtype=jnp.int32)[None, :]
    return jnp.sum(jnp.where(hit, table[None, :], 0), axis=1)


def delay_plan(sub_dev, held, tm_bits, freq_bits, shared, all_trials):
    terms = 1 + tm_bits + freq_bits
    local_bits = sub_dev.bit_length() - 1
    held_bits = held.bit_length() - 1

    def held_trial(m, right):
        value = np.zeros(terms, np.int64)
        for p in range(held_bits + tm_bits):
            if p < right:
                continue
            if p < held_bits:
                value[0] += (m >> p & 1) << (p - right)
            else:
                value[1 + p - held_bits] += 1 << (p - right)
        return value

    ids, rates, jits = [], [], []
    slot = {}
    for k in range(1, local_bits + 1):
        trial_count = 2**k
        for m in range(held):
            trial = held_trial(m, local_bits - k)
            for g in range(sub_dev >> k):
                key = (k, g, tuple(trial))
                if key in slot:
                    continue
                slot[key] = len(ids)
                rate = np.zeros(terms, np.int64)
                rate[0] = all_trials // trial_count - 1 + g
                for bit in range(freq_bits):
                    rate[1 + tm_bits + bit] = (sub_dev >> k) << bit
                jit = trial.copy()
                jit[0] += trial_count - 2
                ids.append(trial)
                rates.append(rate)
                jits.append(jit)
    paths = np.zeros((held * sub_dev, len(ids)), np.float32)
    for m in range(held):
        for i in range(sub_dev):
            for k in range(1, local_bits + 1):
                if i >> (k - 1) & 1:
                    key = (k, i >> k, tuple(held_trial(m, local_bits - k)))
                    paths[m * sub_dev + i, slot[key]] += 1.0
    unique_count = len(ids)
    level_rows = []
    now = np.zeros((held, terms), np.int64)
    for m in range(held):
        now[m] = held_trial(m, 0)
    for bit_index in range(freq_bits):
        trial_count = sub_dev * 2 ** (bit_index + 1)
        if bit_index >= freq_bits - shared:
            now = 2 * np.repeat(now, 2, axis=0)
            now[:, 0] = now[:, 0] + np.tile(np.arange(2), now.shape[0] // 2)
        else:
            now = 2 * now
            now[:, 1 + tm_bits + bit_index] = now[:, 1 + tm_bits + bit_index] + 1
        rate = np.zeros(terms, np.int64)
        rate[0] = all_trials // trial_count - 1
        for bit in range(bit_index + 1, freq_bits):
            rate[1 + tm_bits + bit] = 1 << (bit - bit_index - 1)
        for row in now:
            jit = row.copy()
            jit[0] += trial_count - 2
            ids.append(row.copy())
            rates.append(rate)
            jits.append(jit)
        level_rows.append(now.shape[0])
    pack = lambda parts: np.stack(parts, axis=1).astype(np.int32)
    return pack(ids), pack(rates), pack(jits), paths, unique_count, level_rows


def shards(spectrogram, low_share, jitter):
    sub_dev = spectrogram.shape[0] // SUMMED
    span_time = spectrogram.shape[1]
    all_trials = low_share.shape[0] + 1
    freq_bits = lax.axis_size("freq").bit_length() - 1
    tm_count = lax.axis_size("tm")
    shared = min(SHARED_LEVELS, freq_bits)
    device = lax.axis_index("freq")
    place = lax.axis_index("tm")
    held = sub_dev // tm_count

    tm_bits = tm_count.bit_length() - 1
    id_terms, rate_terms, jitter_terms, paths, unique_count, level_rows = delay_plan(
        sub_dev, held, tm_bits, freq_bits, shared, all_trials
    )
    factors = jnp.concatenate(
        [jnp.ones((1,), jnp.int32),
         (place >> jnp.arange(tm_bits, dtype=jnp.int32) & 1).astype(jnp.int32),
         (device >> jnp.arange(freq_bits, dtype=jnp.int32) & 1).astype(jnp.int32)]
    )[:, None]
    ids_all = jnp.sum(factors * id_terms, axis=0)
    rates = picked(low_share, jnp.sum(factors * rate_terms, axis=0))
    jitters = picked(jitter, jnp.sum(factors * jitter_terms, axis=0))
    shift_table = (ids_all * rates + jitters) // 64
    path_shift = jnp.dot(
        paths, shift_table[:unique_count].astype(jnp.float32), precision=lax.Precision.HIGHEST
    )
    path_shift = jnp.round(path_shift).astype(jnp.int32)
    level_shifts = []
    start = unique_count
    for rows in level_rows:
        level_shifts.append(shift_table[start : start + rows])
        start = start + rows

    base = jnp.sum(spectrogram.reshape(sub_dev, SUMMED, span_time), axis=1, dtype=jnp.float32)
    spread = jnp.broadcast_to(base[None], (tm_count,) + base.shape)
    gathered = lax.all_to_all(spread, "tm", 0, 0, tiled=True)
    base = jnp.transpose(gathered, (1, 0, 2)).reshape(sub_dev, tm_count * span_time)
    full_time = base.shape[1]
    local_limit = sum(2**k - 1 for k in range(1, sub_dev.bit_length()))
    moved = shift_rows(jnp.tile(base, (held, 1)), path_shift, max(local_limit.bit_length(), 1))
    trial_rows = jnp.sum(moved.reshape(held, sub_dev, full_time), axis=1)
    level = 0
    for bit_index in range(freq_bits):
        need_now = sub_dev * 2 ** (bit_index + 1) - 1
        if bit_index == freq_bits - 1 and shared >= 3 and bit_index >= 2:
            partner = paired(trial_rows, "freq", near_half(bit_index, bit_index - 2))
        else:
            partner = swapped(trial_rows, "freq", bit_index)
        upper_half = device >> bit_index & 1
        low_rows = jnp.where(upper_half == 1, partner, trial_rows)
        high_rows = jnp.where(upper_half == 1, trial_rows, partner)
        if bit_index >= freq_bits - shared:
            low_rows = jnp.repeat(low_rows, 2, axis=0)
            high_rows = jnp.repeat(high_rows, 2, axis=0)
        trial_rows = merge_rows(
            low_rows, zero_front(high_rows, need_now), level_shifts[level], need_now
        )
        level = level + 1
    signal = trial_rows / math.sqrt(all_trials * SUMMED)
    peak_rows = []
    window_sum = signal
    width_now = 1
    for level_index in range(WIDTHS):
        peak_rows.append(jnp.max(window_sum, axis=0) / math.sqrt(width_now))
        if level_index + 1 < WIDTHS:
            window_sum = window_sum + zero_front(window_sum, width_now)[:, :full_time]
            width_now = width_now * 2
    best = jnp.stack(peak_rows).reshape(WIDTHS, tm_count, span_time)
    best = jnp.max(lax.all_to_all(best, "tm", 1, 1, tiled=True), axis=1)
    for bit_index in range(freq_bits - shared):
        if bit_index == 3:
            best = jnp.maximum(best, paired(best, "freq", near_half(bit_index, 1)))
        else:
            best = jnp.maximum(best, swapped(best, "freq", bit_index))
    return best


def solution(mesh):
    placed = (P("freq", "tm"), P(), P())
    return jax.shard_map(
        shards, mesh=mesh, in_specs=placed, out_specs=P(None, "tm"), check_vma=False
    )
```

```python
import math

import numpy as np
import jax
import jax.numpy as jnp
from jax import lax
from jax.sharding import PartitionSpec as P

SUMMED = 32
WIDTHS = 9
SHARED_LEVELS = 3
NEAR_HALF = (6, 7, 4, 5, 2, 3, 0, 1)


def swapped(block, axis, apart):
    count = lax.axis_size(axis)
    route = []
    for low in range(count):
        high = low | 1 << apart
        if high != low and high < count:
            route += [(low, high), (high, low)]
    return lax.ppermute(block, axis, route)


def paired(block, axis, partner_of):
    return lax.ppermute(block, axis, [(partner_of(i), i) for i in range(lax.axis_size(axis))])


def near_half(bit_index, ring_bits):
    def partner_of(i):
        ring = i >> ring_bits & 7
        return i - (ring << ring_bits) + (NEAR_HALF[ring] << ring_bits)

    return partner_of


def zero_front(rows, width):
    return jnp.pad(rows, [(0, 0)] * (rows.ndim - 1) + [(width, 0)])


def merge_rows(low_rows, high_rows, shifts, need_now):
    offsets = need_now - shifts
    bit_count = max(need_now.bit_length(), 1)
    moved = high_rows
    for bit_index in range(bit_count):
        step_size = 2**bit_index
        cols = moved.shape[-1]
        selected = (offsets >> bit_index & 1)[:, None] == 1
        moved = jnp.where(selected, moved[:, step_size:], moved[:, : cols - step_size])
    return low_rows + moved


def shift_rows(rows, shifts, bit_count):
    limit = 2**bit_count - 1
    offsets = limit - shifts
    moved = zero_front(rows, limit)
    for bit_index in range(bit_count):
        step_size = 2**bit_index
        cols = moved.shape[-1]
        selected = (offsets >> bit_index & 1)[:, None] == 1
        moved = jnp.where(selected, moved[:, step_size:], moved[:, : cols - step_size])
    return moved


def picked(table, index):
    hit = index[:, None] == jnp.arange(table.shape[0], dtype=jnp.int32)[None, :]
    return jnp.sum(jnp.where(hit, table[None, :], 0), axis=1)


def delay_plan(sub_dev, held, tm_bits, freq_bits, shared, all_trials):
    terms = 1 + tm_bits + freq_bits
    local_bits = sub_dev.bit_length() - 1
    held_bits = held.bit_length() - 1

    def held_trial(m, right):
        value = np.zeros(terms, np.int64)
        for p in range(held_bits + tm_bits):
            if p < right:
                continue
            if p < held_bits:
                value[0] += (m >> p & 1) << (p - right)
            else:
                value[1 + p - held_bits] += 1 << (p - right)
        return value

    ids, rates, jits = [], [], []
    slot = {}
    for k in range(1, local_bits + 1):
        trial_count = 2**k
        for d in range(sub_dev):
            for g in range(sub_dev >> k):
                key = (k, g, d >> (local_bits - k))
                if key in slot:
                    continue
                slot[key] = len(ids)
                trial = np.zeros(terms, np.int64)
                trial[0] = d >> (local_bits - k)
                rate = np.zeros(terms, np.int64)
                rate[0] = all_trials // trial_count - 1 + g
                for bit in range(freq_bits):
                    rate[1 + tm_bits + bit] = (sub_dev >> k) << bit
                jit = trial.copy()
                jit[0] += trial_count - 2
                ids.append(trial)
                rates.append(rate)
                jits.append(jit)
    paths = np.zeros((sub_dev * sub_dev, len(ids)), np.float32)
    for d in range(sub_dev):
        for i in range(sub_dev):
            for k in range(1, local_bits + 1):
                if i >> (k - 1) & 1:
                    paths[d * sub_dev + i, slot[(k, i >> k, d >> (local_bits - k))]] += 1.0
    unique_count = len(ids)
    level_rows = []
    now = np.zeros((held, terms), np.int64)
    for m in range(held):
        now[m] = held_trial(m, 0)
    for bit_index in range(freq_bits):
        trial_count = sub_dev * 2 ** (bit_index + 1)
        if bit_index >= freq_bits - shared:
            now = 2 * np.repeat(now, 2, axis=0)
            now[:, 0] = now[:, 0] + np.tile(np.arange(2), now.shape[0] // 2)
        else:
            now = 2 * now
            now[:, 1 + tm_bits + bit_index] = now[:, 1 + tm_bits + bit_index] + 1
        rate = np.zeros(terms, np.int64)
        rate[0] = all_trials // trial_count - 1
        for bit in range(bit_index + 1, freq_bits):
            rate[1 + tm_bits + bit] = 1 << (bit - bit_index - 1)
        for row in now:
            jit = row.copy()
            jit[0] += trial_count - 2
            ids.append(row.copy())
            rates.append(rate)
            jits.append(jit)
        level_rows.append(now.shape[0])
    pack = lambda parts: np.stack(parts, axis=1).astype(np.int32)
    return pack(ids), pack(rates), pack(jits), paths, unique_count, level_rows


def shards(spectrogram, low_share, jitter):
    sub_dev = spectrogram.shape[0] // SUMMED
    span_time = spectrogram.shape[1]
    all_trials = low_share.shape[0] + 1
    freq_bits = lax.axis_size("freq").bit_length() - 1
    tm_count = lax.axis_size("tm")
    shared = min(SHARED_LEVELS, freq_bits)
    device = lax.axis_index("freq")
    place = lax.axis_index("tm")
    held = sub_dev // tm_count

    tm_bits = tm_count.bit_length() - 1
    id_terms, rate_terms, jitter_terms, paths, unique_count, level_rows = delay_plan(
        sub_dev, held, tm_bits, freq_bits, shared, all_trials
    )
    factors = jnp.concatenate(
        [jnp.ones((1,), jnp.int32),
         (place >> jnp.arange(tm_bits, dtype=jnp.int32) & 1).astype(jnp.int32),
         (device >> jnp.arange(freq_bits, dtype=jnp.int32) & 1).astype(jnp.int32)]
    )[:, None]
    ids_all = jnp.sum(factors * id_terms, axis=0)
    rates = picked(low_share, jnp.sum(factors * rate_terms, axis=0))
    jitters = picked(jitter, jnp.sum(factors * jitter_terms, axis=0))
    shift_table = (ids_all * rates + jitters) // 64
    path_shift = jnp.dot(
        paths, shift_table[:unique_count].astype(jnp.float32), precision=lax.Precision.HIGHEST
    )
    path_shift = jnp.round(path_shift).astype(jnp.int32)
    level_shifts = []
    start = unique_count
    for rows in level_rows:
        level_shifts.append(shift_table[start : start + rows])
        start = start + rows

    base = jnp.sum(spectrogram.reshape(sub_dev, SUMMED, span_time), axis=1, dtype=jnp.float32)
    full_time = tm_count * span_time
    halo = sum(2**k - 1 for k in range(1, sub_dev.bit_length()))
    width = span_time + halo
    padded = jnp.pad(base, ((0, 0), (0, halo)))
    moved = shift_rows(jnp.tile(padded, (sub_dev, 1)), path_shift, max(halo.bit_length(), 1))
    partial = jnp.sum(moved.reshape(sub_dev, sub_dev, width), axis=1)
    arrived = lax.all_to_all(partial.reshape(tm_count, held, width), "tm", 0, 0, tiled=True)
    main = jnp.transpose(arrived[:, :, :span_time], (1, 0, 2)).reshape(held, full_time)
    spill = jnp.pad(arrived[:-1, :, span_time:], ((1, 0), (0, 0), (0, span_time - halo)))
    trial_rows = main + jnp.transpose(spill, (1, 0, 2)).reshape(held, full_time)
    level = 0
    for bit_index in range(freq_bits):
        need_now = sub_dev * 2 ** (bit_index + 1) - 1
        if bit_index == freq_bits - 1 and shared >= 3 and bit_index >= 2:
            partner = paired(trial_rows, "freq", near_half(bit_index, bit_index - 2))
        else:
            partner = swapped(trial_rows, "freq", bit_index)
        upper_half = device >> bit_index & 1
        low_rows = jnp.where(upper_half == 1, partner, trial_rows)
        high_rows = jnp.where(upper_half == 1, trial_rows, partner)
        if bit_index >= freq_bits - shared:
            low_rows = jnp.repeat(low_rows, 2, axis=0)
            high_rows = jnp.repeat(high_rows, 2, axis=0)
        trial_rows = merge_rows(
            low_rows, zero_front(high_rows, need_now), level_shifts[level], need_now
        )
        level = level + 1
    signal = trial_rows / math.sqrt(all_trials * SUMMED)
    peak_rows = []
    window_sum = signal
    width_now = 1
    for level_index in range(WIDTHS):
        peak_rows.append(jnp.max(window_sum, axis=0) / math.sqrt(width_now))
        if level_index + 1 < WIDTHS:
            window_sum = window_sum + zero_front(window_sum, width_now)[:, :full_time]
            width_now = width_now * 2
    best = jnp.stack(peak_rows).reshape(WIDTHS, tm_count, span_time)
    best = jnp.max(lax.all_to_all(best, "tm", 1, 1, tiled=True), axis=1)
    for bit_index in range(freq_bits - shared):
        if bit_index == 3:
            best = jnp.maximum(best, paired(best, "freq", near_half(bit_index, 1)))
        else:
            best = jnp.maximum(best, swapped(best, "freq", bit_index))
    return best


def solution(mesh):
    placed = (P("freq", "tm"), P(), P())
    return jax.shard_map(
        shards, mesh=mesh, in_specs=placed, out_specs=P(None, "tm"), check_vma=False
    )
```

```python
import functools
import math

import numpy as np
import jax
import jax.numpy as jnp
from jax import lax
from jax.sharding import PartitionSpec as P

SUMMED = 32
WIDTHS = 9
SHARED_LEVELS = 3
NEAR_HALF = (6, 7, 4, 5, 2, 3, 0, 1)
FINE_AXES = ("fy", "zh", "zl", "fc")


def swapped(block, axis, apart):
    count = lax.axis_size(axis)
    route = []
    for low in range(count):
        high = low | 1 << apart
        if high != low and high < count:
            route += [(low, high), (high, low)]
    return lax.ppermute(block, axis, route)


def paired(block, axis, partner_of):
    return lax.ppermute(block, axis, [(partner_of(i), i) for i in range(lax.axis_size(axis))])


def near_half(bit_index, ring_bits):
    def partner_of(i):
        ring = i >> ring_bits & 7
        return i - (ring << ring_bits) + (NEAR_HALF[ring] << ring_bits)

    return partner_of


def zero_front(rows, width):
    return jnp.pad(rows, [(0, 0)] * (rows.ndim - 1) + [(width, 0)])


def merge_rows(low_rows, high_rows, shifts, need_now):
    offsets = need_now - shifts
    bit_count = max(need_now.bit_length(), 1)
    moved = high_rows
    for bit_index in range(bit_count):
        step_size = 2**bit_index
        cols = moved.shape[-1]
        selected = (offsets >> bit_index & 1)[:, None] == 1
        moved = jnp.where(selected, moved[:, step_size:], moved[:, : cols - step_size])
    return low_rows + moved


def shift_rows(rows, shifts, bit_count):
    limit = 2**bit_count - 1
    offsets = limit - shifts
    moved = zero_front(rows, limit)
    for bit_index in range(bit_count):
        step_size = 2**bit_index
        cols = moved.shape[-1]
        selected = (offsets >> bit_index & 1)[:, None] == 1
        moved = jnp.where(selected, moved[:, step_size:], moved[:, : cols - step_size])
    return moved


def picked(table, index):
    hit = index[:, None] == jnp.arange(table.shape[0], dtype=jnp.int32)[None, :]
    return jnp.sum(jnp.where(hit, table[None, :], 0), axis=1)


def delay_plan(sub_dev, held, tm_bits, freq_bits, shared, all_trials):
    terms = 1 + tm_bits + freq_bits
    local_bits = sub_dev.bit_length() - 1
    held_bits = held.bit_length() - 1

    def held_trial(m, right):
        value = np.zeros(terms, np.int64)
        for p in range(held_bits + tm_bits):
            if p < right:
                continue
            if p < held_bits:
                value[0] += (m >> p & 1) << (p - right)
            else:
                value[1 + p - held_bits] += 1 << (p - right)
        return value

    ids, rates, jits = [], [], []
    slot = {}
    for k in range(1, local_bits + 1):
        trial_count = 2**k
        for m in range(held):
            trial = held_trial(m, local_bits - k)
            for g in range(sub_dev >> k):
                key = (k, g, tuple(trial))
                if key in slot:
                    continue
                slot[key] = len(ids)
                rate = np.zeros(terms, np.int64)
                rate[0] = all_trials // trial_count - 1 + g
                for bit in range(freq_bits):
                    rate[1 + tm_bits + bit] = (sub_dev >> k) << bit
                jit = trial.copy()
                jit[0] += trial_count - 2
                ids.append(trial)
                rates.append(rate)
                jits.append(jit)
    paths = np.zeros((held * sub_dev, len(ids)), np.float32)
    for m in range(held):
        for i in range(sub_dev):
            for k in range(1, local_bits + 1):
                if i >> (k - 1) & 1:
                    key = (k, i >> k, tuple(held_trial(m, local_bits - k)))
                    paths[m * sub_dev + i, slot[key]] += 1.0
    unique_count = len(ids)
    level_rows = []
    now = np.zeros((held, terms), np.int64)
    for m in range(held):
        now[m] = held_trial(m, 0)
    for bit_index in range(freq_bits):
        trial_count = sub_dev * 2 ** (bit_index + 1)
        if bit_index >= freq_bits - shared:
            now = 2 * np.repeat(now, 2, axis=0)
            now[:, 0] = now[:, 0] + np.tile(np.arange(2), now.shape[0] // 2)
        else:
            now = 2 * now
            now[:, 1 + tm_bits + bit_index] = now[:, 1 + tm_bits + bit_index] + 1
        rate = np.zeros(terms, np.int64)
        rate[0] = all_trials // trial_count - 1
        for bit in range(bit_index + 1, freq_bits):
            rate[1 + tm_bits + bit] = 1 << (bit - bit_index - 1)
        for row in now:
            jit = row.copy()
            jit[0] += trial_count - 2
            ids.append(row.copy())
            rates.append(rate)
            jits.append(jit)
        level_rows.append(now.shape[0])
    pack = lambda parts: np.stack(parts, axis=1).astype(np.int32)
    return pack(ids), pack(rates), pack(jits), paths, unique_count, level_rows


def shards(freq_axis, spectrogram, low_share, jitter):
    sub_dev = spectrogram.shape[0] // SUMMED
    span_time = spectrogram.shape[1]
    all_trials = low_share.shape[0] + 1
    freq_bits = lax.axis_size(freq_axis).bit_length() - 1
    tm_count = lax.axis_size("tm")
    shared = min(SHARED_LEVELS, freq_bits)
    device = lax.axis_index(freq_axis)
    place = lax.axis_index("tm")
    held = sub_dev // tm_count

    tm_bits = tm_count.bit_length() - 1
    id_terms, rate_terms, jitter_terms, paths, unique_count, level_rows = delay_plan(
        sub_dev, held, tm_bits, freq_bits, shared, all_trials
    )
    factors = jnp.concatenate(
        [jnp.ones((1,), jnp.int32),
         (place >> jnp.arange(tm_bits, dtype=jnp.int32) & 1).astype(jnp.int32),
         (device >> jnp.arange(freq_bits, dtype=jnp.int32) & 1).astype(jnp.int32)]
    )[:, None]
    ids_all = jnp.sum(factors * id_terms, axis=0)
    rates = picked(low_share, jnp.sum(factors * rate_terms, axis=0))
    jitters = picked(jitter, jnp.sum(factors * jitter_terms, axis=0))
    shift_table = (ids_all * rates + jitters) // 64
    path_shift = jnp.dot(
        paths, shift_table[:unique_count].astype(jnp.float32), precision=lax.Precision.HIGHEST
    )
    path_shift = jnp.round(path_shift).astype(jnp.int32)
    level_shifts = []
    start = unique_count
    for rows in level_rows:
        level_shifts.append(shift_table[start : start + rows])
        start = start + rows

    base = jnp.sum(spectrogram.reshape(sub_dev, SUMMED, span_time), axis=1, dtype=jnp.float32)
    spread = jnp.broadcast_to(base[None], (tm_count,) + base.shape)
    gathered = lax.all_to_all(spread, "tm", 0, 0, tiled=True)
    base = jnp.transpose(gathered, (1, 0, 2)).reshape(sub_dev, tm_count * span_time)
    full_time = base.shape[1]
    local_limit = sum(2**k - 1 for k in range(1, sub_dev.bit_length()))
    moved = shift_rows(jnp.tile(base, (held, 1)), path_shift, max(local_limit.bit_length(), 1))
    trial_rows = jnp.sum(moved.reshape(held, sub_dev, full_time), axis=1)
    level = 0
    for bit_index in range(freq_bits):
        need_now = sub_dev * 2 ** (bit_index + 1) - 1
        if bit_index == freq_bits - 1 and shared >= 3 and bit_index >= 2:
            partner = paired(trial_rows, freq_axis, near_half(bit_index, bit_index - 2))
        else:
            partner = swapped(trial_rows, freq_axis, bit_index)
        upper_half = device >> bit_index & 1
        low_rows = jnp.where(upper_half == 1, partner, trial_rows)
        high_rows = jnp.where(upper_half == 1, trial_rows, partner)
        if bit_index >= freq_bits - shared:
            low_rows = jnp.repeat(low_rows, 2, axis=0)
            high_rows = jnp.repeat(high_rows, 2, axis=0)
        trial_rows = merge_rows(
            low_rows, zero_front(high_rows, need_now), level_shifts[level], need_now
        )
        level = level + 1
    signal = trial_rows / math.sqrt(all_trials * SUMMED)
    peak_rows = []
    window_sum = signal
    width_now = 1
    for level_index in range(WIDTHS):
        peak_rows.append(jnp.max(window_sum, axis=0) / math.sqrt(width_now))
        if level_index + 1 < WIDTHS:
            window_sum = window_sum + zero_front(window_sum, width_now)[:, :full_time]
            width_now = width_now * 2
    best = jnp.stack(peak_rows).reshape(WIDTHS, tm_count, span_time)
    best = jnp.max(lax.all_to_all(best, "tm", 1, 1, tiled=True), axis=1)
    for bit_index in range(freq_bits - shared):
        if bit_index == 1 and "zl" in freq_axis:
            spread = jnp.broadcast_to(best[None], (4,) + best.shape)
            best = jnp.max(lax.all_to_all(spread, "zl", 0, 0, tiled=True), axis=0)
        elif bit_index == 2 and "zl" in freq_axis:
            continue
        elif bit_index == 3:
            best = jnp.maximum(best, paired(best, freq_axis, near_half(bit_index, 1)))
        else:
            best = jnp.maximum(best, swapped(best, freq_axis, bit_index))
    return best


def solution(mesh):
    count = mesh.shape["freq"]
    if count % 16 == 0:
        fine = jax.sharding.Mesh(
            mesh.devices.reshape(count // 16, 2, 4, 2, mesh.shape["tm"]), FINE_AXES + ("tm",)
        )
        freq_axis = FINE_AXES
    else:
        fine = mesh
        freq_axis = ("freq",)
    placed = (P(freq_axis, "tm"), P(), P())
    return jax.shard_map(
        functools.partial(shards, freq_axis), mesh=fine, in_specs=placed,
        out_specs=P(None, "tm"), check_vma=False,
    )
```

```python
import functools
import math

import numpy as np
import jax
import jax.numpy as jnp
from jax import lax
from jax.sharding import PartitionSpec as P

SUMMED = 32
WIDTHS = 9
SHARED_LEVELS = 3
NEAR_HALF = (6, 7, 4, 5, 2, 3, 0, 1)
FINE_AXES = ("fy", "zh", "zl", "fc")


def swapped(block, axis, apart):
    count = lax.axis_size(axis)
    route = []
    for low in range(count):
        high = low | 1 << apart
        if high != low and high < count:
            route += [(low, high), (high, low)]
    return lax.ppermute(block, axis, route)


def paired(block, axis, partner_of):
    return lax.ppermute(block, axis, [(partner_of(i), i) for i in range(lax.axis_size(axis))])


def near_half(bit_index, ring_bits):
    def partner_of(i):
        ring = i >> ring_bits & 7
        return i - (ring << ring_bits) + (NEAR_HALF[ring] << ring_bits)

    return partner_of


def zero_front(rows, width):
    return jnp.pad(rows, [(0, 0)] * (rows.ndim - 1) + [(width, 0)])


def merge_rows(low_rows, high_rows, shifts, need_now):
    offsets = need_now - shifts
    bit_count = max(need_now.bit_length(), 1)
    moved = high_rows
    for bit_index in range(bit_count):
        step_size = 2**bit_index
        cols = moved.shape[-1]
        selected = (offsets >> bit_index & 1)[:, None] == 1
        moved = jnp.where(selected, moved[:, step_size:], moved[:, : cols - step_size])
    return low_rows + moved


def shift_rows(rows, shifts, bit_count):
    limit = 2**bit_count - 1
    offsets = limit - shifts
    moved = zero_front(rows, limit)
    for bit_index in range(bit_count):
        step_size = 2**bit_index
        cols = moved.shape[-1]
        selected = (offsets >> bit_index & 1)[:, None] == 1
        moved = jnp.where(selected, moved[:, step_size:], moved[:, : cols - step_size])
    return moved


def picked(table, index):
    hit = index[:, None] == jnp.arange(table.shape[0], dtype=jnp.int32)[None, :]
    return jnp.sum(jnp.where(hit, table[None, :], 0), axis=1)


def delay_plan(sub_dev, held, tm_bits, freq_bits, shared, all_trials, pair_bit):
    terms = 1 + tm_bits + freq_bits
    local_bits = sub_dev.bit_length() - 1
    held_bits = held.bit_length() - 1

    def held_trial(m, right):
        value = np.zeros(terms, np.int64)
        for p in range(held_bits + tm_bits):
            if p < right:
                continue
            if p < held_bits:
                value[0] += (m >> p & 1) << (p - right)
            else:
                value[1 + p - held_bits] += 1 << (p - right)
        return value

    ids, rates, jits = [], [], []
    slot = {}
    for k in range(1, local_bits + 1):
        trial_count = 2**k
        for m in range(held):
            trial = held_trial(m, local_bits - k)
            for g in range(sub_dev >> k):
                key = (k, g, tuple(trial))
                if key in slot:
                    continue
                slot[key] = len(ids)
                rate = np.zeros(terms, np.int64)
                rate[0] = all_trials // trial_count - 1 + g
                for bit in range(freq_bits):
                    rate[1 + tm_bits + bit] = (sub_dev >> k) << bit
                jit = trial.copy()
                jit[0] += trial_count - 2
                ids.append(trial)
                rates.append(rate)
                jits.append(jit)
    paths = np.zeros((held * sub_dev, len(ids)), np.float32)
    for m in range(held):
        for i in range(sub_dev):
            for k in range(1, local_bits + 1):
                if i >> (k - 1) & 1:
                    key = (k, i >> k, tuple(held_trial(m, local_bits - k)))
                    paths[m * sub_dev + i, slot[key]] += 1.0
    unique_count = len(ids)
    level_rows = []
    now = np.zeros((held, terms), np.int64)
    for m in range(held):
        now[m] = held_trial(m, 0)
    for bit_index in range(freq_bits):
        trial_count = sub_dev * 2 ** (bit_index + 1)
        if bit_index >= freq_bits - shared:
            now = 2 * np.repeat(now, 2, axis=0)
            now[:, 0] = now[:, 0] + np.tile(np.arange(2), now.shape[0] // 2)
        else:
            now = 2 * now
            now[:, 1 + tm_bits + bit_index] = now[:, 1 + tm_bits + bit_index] + 1
        rate = np.zeros(terms, np.int64)
        rate[0] = all_trials // trial_count - 1
        for bit in range(bit_index + 1, freq_bits):
            rate[1 + tm_bits + bit] = 1 << (bit - bit_index - 1)
        choices = [rate]
        if bit_index == pair_bit:
            choices = []
            for half in range(2):
                one = rate.copy()
                one[1 + tm_bits + bit_index + 1] = 0
                one[0] += half
                choices.append(one)
        for one in choices:
            for row in now:
                jit = row.copy()
                jit[0] += trial_count - 2
                ids.append(row.copy())
                rates.append(one)
                jits.append(jit)
        level_rows.append(now.shape[0] * len(choices))
    pack = lambda parts: np.stack(parts, axis=1).astype(np.int32)
    return pack(ids), pack(rates), pack(jits), paths, unique_count, level_rows


def shards(freq_axis, spectrogram, low_share, jitter):
    sub_dev = spectrogram.shape[0] // SUMMED
    span_time = spectrogram.shape[1]
    all_trials = low_share.shape[0] + 1
    freq_bits = lax.axis_size(freq_axis).bit_length() - 1
    tm_count = lax.axis_size("tm")
    shared = min(SHARED_LEVELS, freq_bits)
    device = lax.axis_index(freq_axis)
    place = lax.axis_index("tm")
    held = sub_dev // tm_count

    tm_bits = tm_count.bit_length() - 1
    pair_bit = 1 if "zl" in freq_axis and freq_bits - shared > 2 else -1
    id_terms, rate_terms, jitter_terms, paths, unique_count, level_rows = delay_plan(
        sub_dev, held, tm_bits, freq_bits, shared, all_trials, pair_bit
    )
    factors = jnp.concatenate(
        [jnp.ones((1,), jnp.int32),
         (place >> jnp.arange(tm_bits, dtype=jnp.int32) & 1).astype(jnp.int32),
         (device >> jnp.arange(freq_bits, dtype=jnp.int32) & 1).astype(jnp.int32)]
    )[:, None]
    ids_all = jnp.sum(factors * id_terms, axis=0)
    rates = picked(low_share, jnp.sum(factors * rate_terms, axis=0))
    jitters = picked(jitter, jnp.sum(factors * jitter_terms, axis=0))
    shift_table = (ids_all * rates + jitters) // 64
    path_shift = jnp.dot(
        paths, shift_table[:unique_count].astype(jnp.float32), precision=lax.Precision.HIGHEST
    )
    path_shift = jnp.round(path_shift).astype(jnp.int32)
    level_shifts = []
    start = unique_count
    for rows in level_rows:
        level_shifts.append(shift_table[start : start + rows])
        start = start + rows

    base = jnp.sum(spectrogram.reshape(sub_dev, SUMMED, span_time), axis=1, dtype=jnp.float32)
    spread = jnp.broadcast_to(base[None], (tm_count,) + base.shape)
    gathered = lax.all_to_all(spread, "tm", 0, 0, tiled=True)
    base = jnp.transpose(gathered, (1, 0, 2)).reshape(sub_dev, tm_count * span_time)
    full_time = base.shape[1]
    local_limit = sum(2**k - 1 for k in range(1, sub_dev.bit_length()))
    moved = shift_rows(jnp.tile(base, (held, 1)), path_shift, max(local_limit.bit_length(), 1))
    trial_rows = jnp.sum(moved.reshape(held, sub_dev, full_time), axis=1)
    level = 0
    for bit_index in range(freq_bits):
        need_now = sub_dev * 2 ** (bit_index + 1) - 1
        if bit_index == pair_bit:
            spread = jnp.broadcast_to(trial_rows[None], (4,) + trial_rows.shape)
            peers = lax.all_to_all(spread, "zl", 0, 0, tiled=True)
            pairs = merge_rows(
                jnp.concatenate([peers[0], peers[2]], axis=0),
                zero_front(jnp.concatenate([peers[1], peers[3]], axis=0), need_now),
                level_shifts[level],
                need_now,
            )
            held_rows = trial_rows.shape[0]
            level = level + 1
            need_next = 2 * need_now + 1
            trial_rows = merge_rows(
                pairs[:held_rows], zero_front(pairs[held_rows:], need_next),
                level_shifts[level], need_next,
            )
            level = level + 1
            continue
        if pair_bit >= 0 and bit_index == pair_bit + 1:
            continue
        if bit_index == freq_bits - 1 and shared >= 3 and bit_index >= 2:
            partner = paired(trial_rows, freq_axis, near_half(bit_index, bit_index - 2))
        else:
            partner = swapped(trial_rows, freq_axis, bit_index)
        upper_half = device >> bit_index & 1
        low_rows = jnp.where(upper_half == 1, partner, trial_rows)
        high_rows = jnp.where(upper_half == 1, trial_rows, partner)
        if bit_index >= freq_bits - shared:
            low_rows = jnp.repeat(low_rows, 2, axis=0)
            high_rows = jnp.repeat(high_rows, 2, axis=0)
        trial_rows = merge_rows(
            low_rows, zero_front(high_rows, need_now), level_shifts[level], need_now
        )
        level = level + 1
    signal = trial_rows / math.sqrt(all_trials * SUMMED)
    peak_rows = []
    window_sum = signal
    width_now = 1
    for level_index in range(WIDTHS):
        peak_rows.append(jnp.max(window_sum, axis=0) / math.sqrt(width_now))
        if level_index + 1 < WIDTHS:
            window_sum = window_sum + zero_front(window_sum, width_now)[:, :full_time]
            width_now = width_now * 2
    best = jnp.stack(peak_rows).reshape(WIDTHS, tm_count, span_time)
    best = jnp.max(lax.all_to_all(best, "tm", 1, 1, tiled=True), axis=1)
    for bit_index in range(freq_bits - shared):
        if bit_index == 1 and "zl" in freq_axis:
            spread = jnp.broadcast_to(best[None], (4,) + best.shape)
            best = jnp.max(lax.all_to_all(spread, "zl", 0, 0, tiled=True), axis=0)
        elif bit_index == 2 and "zl" in freq_axis:
            continue
        elif bit_index == 3:
            best = jnp.maximum(best, paired(best, freq_axis, near_half(bit_index, 1)))
        else:
            best = jnp.maximum(best, swapped(best, freq_axis, bit_index))
    return best


def solution(mesh):
    count = mesh.shape["freq"]
    if count % 16 == 0:
        fine = jax.sharding.Mesh(
            mesh.devices.reshape(count // 16, 2, 4, 2, mesh.shape["tm"]), FINE_AXES + ("tm",)
        )
        freq_axis = FINE_AXES
    else:
        fine = mesh
        freq_axis = ("freq",)
    placed = (P(freq_axis, "tm"), P(), P())
    return jax.shard_map(
        functools.partial(shards, freq_axis), mesh=fine, in_specs=placed,
        out_specs=P(None, "tm"), check_vma=False,
    )
```

```python
import functools
import math

import numpy as np
import jax
import jax.numpy as jnp
from jax import lax
from jax.sharding import PartitionSpec as P

SUMMED = 32
WIDTHS = 9
SHARED_LEVELS = 3
NEAR_HALF = (6, 7, 4, 5, 2, 3, 0, 1)


def swapped(block, axis, apart):
    count = lax.axis_size(axis)
    route = []
    for low in range(count):
        high = low | 1 << apart
        if high != low and high < count:
            route += [(low, high), (high, low)]
    return lax.ppermute(block, axis, route)


def paired(block, axis, partner_of):
    return lax.ppermute(block, axis, [(partner_of(i), i) for i in range(lax.axis_size(axis))])


def near_half(bit_index, ring_bits):
    def partner_of(i):
        ring = i >> ring_bits & 7
        return i - (ring << ring_bits) + (NEAR_HALF[ring] << ring_bits)

    return partner_of


def zero_front(rows, width):
    return jnp.pad(rows, [(0, 0)] * (rows.ndim - 1) + [(width, 0)])


def merge_rows(low_rows, high_rows, shifts, need_now):
    offsets = need_now - shifts
    bit_count = max(need_now.bit_length(), 1)
    moved = high_rows
    for bit_index in range(bit_count):
        step_size = 2**bit_index
        cols = moved.shape[-1]
        selected = (offsets >> bit_index & 1)[:, None] == 1
        moved = jnp.where(selected, moved[:, step_size:], moved[:, : cols - step_size])
    return low_rows + moved


def shift_rows(rows, shifts, bit_count):
    limit = 2**bit_count - 1
    offsets = limit - shifts
    moved = zero_front(rows, limit)
    for bit_index in range(bit_count):
        step_size = 2**bit_index
        cols = moved.shape[-1]
        selected = (offsets >> bit_index & 1)[:, None] == 1
        moved = jnp.where(selected, moved[:, step_size:], moved[:, : cols - step_size])
    return moved


def picked(table, index):
    hit = index[:, None] == jnp.arange(table.shape[0], dtype=jnp.int32)[None, :]
    return jnp.sum(jnp.where(hit, table[None, :], 0), axis=1)


def delay_plan(sub_dev, held, tm_bits, freq_bits, shared, all_trials, pair_bits):
    terms = 1 + tm_bits + freq_bits
    local_bits = sub_dev.bit_length() - 1
    held_bits = held.bit_length() - 1

    def held_trial(m, right):
        value = np.zeros(terms, np.int64)
        for p in range(held_bits + tm_bits):
            if p < right:
                continue
            if p < held_bits:
                value[0] += (m >> p & 1) << (p - right)
            else:
                value[1 + p - held_bits] += 1 << (p - right)
        return value

    ids, rates, jits = [], [], []
    slot = {}
    for k in range(1, local_bits + 1):
        trial_count = 2**k
        for m in range(held):
            trial = held_trial(m, local_bits - k)
            for g in range(sub_dev >> k):
                key = (k, g, tuple(trial))
                if key in slot:
                    continue
                slot[key] = len(ids)
                rate = np.zeros(terms, np.int64)
                rate[0] = all_trials // trial_count - 1 + g
                for bit in range(freq_bits):
                    rate[1 + tm_bits + bit] = (sub_dev >> k) << bit
                jit = trial.copy()
                jit[0] += trial_count - 2
                ids.append(trial)
                rates.append(rate)
                jits.append(jit)
    paths = np.zeros((held * sub_dev, len(ids)), np.float32)
    for m in range(held):
        for i in range(sub_dev):
            for k in range(1, local_bits + 1):
                if i >> (k - 1) & 1:
                    key = (k, i >> k, tuple(held_trial(m, local_bits - k)))
                    paths[m * sub_dev + i, slot[key]] += 1.0
    unique_count = len(ids)
    level_rows = []
    now = np.zeros((held, terms), np.int64)
    for m in range(held):
        now[m] = held_trial(m, 0)
    for bit_index in range(freq_bits):
        trial_count = sub_dev * 2 ** (bit_index + 1)
        if bit_index >= freq_bits - shared:
            now = 2 * np.repeat(now, 2, axis=0)
            now[:, 0] = now[:, 0] + np.tile(np.arange(2), now.shape[0] // 2)
        else:
            now = 2 * now
            now[:, 1 + tm_bits + bit_index] = now[:, 1 + tm_bits + bit_index] + 1
        rate = np.zeros(terms, np.int64)
        rate[0] = all_trials // trial_count - 1
        for bit in range(bit_index + 1, freq_bits):
            rate[1 + tm_bits + bit] = 1 << (bit - bit_index - 1)
        choices = [rate]
        if bit_index in pair_bits:
            choices = []
            for half in range(2):
                one = rate.copy()
                one[1 + tm_bits + bit_index + 1] = 0
                one[0] += half
                choices.append(one)
        for one in choices:
            for row in now:
                jit = row.copy()
                jit[0] += trial_count - 2
                ids.append(row.copy())
                rates.append(one)
                jits.append(jit)
        level_rows.append(now.shape[0] * len(choices))
    pack = lambda parts: np.stack(parts, axis=1).astype(np.int32)
    return pack(ids), pack(rates), pack(jits), paths, unique_count, level_rows


def shards(freq_axis, spectrogram, low_share, jitter):
    sub_dev = spectrogram.shape[0] // SUMMED
    span_time = spectrogram.shape[1]
    all_trials = low_share.shape[0] + 1
    freq_bits = lax.axis_size(freq_axis).bit_length() - 1
    tm_count = lax.axis_size("tm")
    shared = min(SHARED_LEVELS, freq_bits)
    device = lax.axis_index(freq_axis)
    place = lax.axis_index("tm")
    held = sub_dev // tm_count

    tm_bits = tm_count.bit_length() - 1
    pair_axes = {}
    for bit_index, name in ((1, "zl"), (4, "yl")):
        redundant = [bit_index + step >= freq_bits - shared for step in (0, 1)]
        if name in freq_axis and redundant[0] == redundant[1]:
            pair_axes[bit_index] = name
    pair_bits = tuple(pair_axes)
    id_terms, rate_terms, jitter_terms, paths, unique_count, level_rows = delay_plan(
        sub_dev, held, tm_bits, freq_bits, shared, all_trials, pair_bits
    )
    factors = jnp.concatenate(
        [jnp.ones((1,), jnp.int32),
         (place >> jnp.arange(tm_bits, dtype=jnp.int32) & 1).astype(jnp.int32),
         (device >> jnp.arange(freq_bits, dtype=jnp.int32) & 1).astype(jnp.int32)]
    )[:, None]
    ids_all = jnp.sum(factors * id_terms, axis=0)
    rates = picked(low_share, jnp.sum(factors * rate_terms, axis=0))
    jitters = picked(jitter, jnp.sum(factors * jitter_terms, axis=0))
    shift_table = (ids_all * rates + jitters) // 64
    path_shift = jnp.dot(
        paths, shift_table[:unique_count].astype(jnp.float32), precision=lax.Precision.HIGHEST
    )
    path_shift = jnp.round(path_shift).astype(jnp.int32)
    level_shifts = []
    start = unique_count
    for rows in level_rows:
        level_shifts.append(shift_table[start : start + rows])
        start = start + rows

    base = jnp.sum(spectrogram.reshape(sub_dev, SUMMED, span_time), axis=1, dtype=jnp.float32)
    spread = jnp.broadcast_to(base[None], (tm_count,) + base.shape)
    gathered = lax.all_to_all(spread, "tm", 0, 0, tiled=True)
    base = jnp.transpose(gathered, (1, 0, 2)).reshape(sub_dev, tm_count * span_time)
    full_time = base.shape[1]
    local_limit = sum(2**k - 1 for k in range(1, sub_dev.bit_length()))
    moved = shift_rows(jnp.tile(base, (held, 1)), path_shift, max(local_limit.bit_length(), 1))
    trial_rows = jnp.sum(moved.reshape(held, sub_dev, full_time), axis=1)
    level = 0
    for bit_index in range(freq_bits):
        need_now = sub_dev * 2 ** (bit_index + 1) - 1
        if bit_index in pair_axes:
            spread = jnp.broadcast_to(trial_rows[None], (4,) + trial_rows.shape)
            peers = lax.all_to_all(spread, pair_axes[bit_index], 0, 0, tiled=True)
            doubled = bit_index >= freq_bits - shared
            if doubled:
                peers = jnp.repeat(peers, 2, axis=1)
            pairs = merge_rows(
                jnp.concatenate([peers[0], peers[2]], axis=0),
                zero_front(jnp.concatenate([peers[1], peers[3]], axis=0), need_now),
                level_shifts[level],
                need_now,
            )
            half = pairs.shape[0] // 2
            low_rows, high_rows = pairs[:half], pairs[half:]
            if doubled:
                low_rows = jnp.repeat(low_rows, 2, axis=0)
                high_rows = jnp.repeat(high_rows, 2, axis=0)
            level = level + 1
            need_next = 2 * need_now + 1
            trial_rows = merge_rows(
                low_rows, zero_front(high_rows, need_next), level_shifts[level], need_next
            )
            level = level + 1
            continue
        if bit_index - 1 in pair_axes:
            continue
        if bit_index == freq_bits - 1 and shared >= 3 and bit_index >= 2:
            partner = paired(trial_rows, freq_axis, near_half(bit_index, bit_index - 2))
        else:
            partner = swapped(trial_rows, freq_axis, bit_index)
        upper_half = device >> bit_index & 1
        low_rows = jnp.where(upper_half == 1, partner, trial_rows)
        high_rows = jnp.where(upper_half == 1, trial_rows, partner)
        if bit_index >= freq_bits - shared:
            low_rows = jnp.repeat(low_rows, 2, axis=0)
            high_rows = jnp.repeat(high_rows, 2, axis=0)
        trial_rows = merge_rows(
            low_rows, zero_front(high_rows, need_now), level_shifts[level], need_now
        )
        level = level + 1
    signal = trial_rows / math.sqrt(all_trials * SUMMED)
    peak_rows = []
    window_sum = signal
    width_now = 1
    for level_index in range(WIDTHS):
        peak_rows.append(jnp.max(window_sum, axis=0) / math.sqrt(width_now))
        if level_index + 1 < WIDTHS:
            window_sum = window_sum + zero_front(window_sum, width_now)[:, :full_time]
            width_now = width_now * 2
    best = jnp.stack(peak_rows).reshape(WIDTHS, tm_count, span_time)
    best = jnp.max(lax.all_to_all(best, "tm", 1, 1, tiled=True), axis=1)
    for bit_index in range(freq_bits - shared):
        if bit_index == 1 and "zl" in freq_axis:
            spread = jnp.broadcast_to(best[None], (4,) + best.shape)
            best = jnp.max(lax.all_to_all(spread, "zl", 0, 0, tiled=True), axis=0)
        elif bit_index == 2 and "zl" in freq_axis:
            continue
        elif bit_index == 3:
            best = jnp.maximum(best, paired(best, freq_axis, near_half(bit_index, 1)))
        else:
            best = jnp.maximum(best, swapped(best, freq_axis, bit_index))
    return best


def solution(mesh):
    count = mesh.shape["freq"]
    if count == 128:
        freq_axis, sizes = ("yh", "yl", "zh", "zl", "fc"), (2, 4, 2, 4, 2)
    elif count == 16:
        freq_axis, sizes = ("zh", "zl", "fc"), (2, 4, 2)
    else:
        freq_axis, sizes = ("freq",), (count,)
    fine = jax.sharding.Mesh(
        mesh.devices.reshape(sizes + (mesh.shape["tm"],)), freq_axis + ("tm",)
    )
    placed = (P(freq_axis, "tm"), P(), P())
    return jax.shard_map(
        functools.partial(shards, freq_axis), mesh=fine, in_specs=placed,
        out_specs=P(None, "tm"), check_vma=False,
    )
```

```python
import functools
import math

import numpy as np
import jax
import jax.numpy as jnp
from jax import lax
from jax.sharding import PartitionSpec as P

SUMMED = 32
WIDTHS = 9
SHARED_LEVELS = 3
NEAR_HALF = (6, 7, 4, 5, 2, 3, 0, 1)
FINE_BITS = {"yh": 1, "yl": 2, "zh": 1, "zl": 2, "fc": 1}


def swapped(block, axis, apart):
    count = lax.axis_size(axis)
    route = []
    for low in range(count):
        high = low | 1 << apart
        if high != low and high < count:
            route += [(low, high), (high, low)]
    return lax.ppermute(block, axis, route)


def paired(block, axis, partner_of):
    return lax.ppermute(block, axis, [(partner_of(i), i) for i in range(lax.axis_size(axis))])


def near_half(bit_index, ring_bits):
    def partner_of(i):
        ring = i >> ring_bits & 7
        return i - (ring << ring_bits) + (NEAR_HALF[ring] << ring_bits)

    return partner_of


def zero_front(rows, width):
    return jnp.pad(rows, [(0, 0)] * (rows.ndim - 1) + [(width, 0)])


def merge_rows(low_rows, high_rows, shifts, need_now):
    offsets = need_now - shifts
    bit_count = max(need_now.bit_length(), 1)
    moved = high_rows
    for bit_index in range(bit_count):
        step_size = 2**bit_index
        cols = moved.shape[-1]
        selected = (offsets >> bit_index & 1)[:, None] == 1
        moved = jnp.where(selected, moved[:, step_size:], moved[:, : cols - step_size])
    return low_rows + moved


def shift_rows(rows, shifts, bit_count):
    limit = 2**bit_count - 1
    offsets = limit - shifts
    moved = zero_front(rows, limit)
    for bit_index in range(bit_count):
        step_size = 2**bit_index
        cols = moved.shape[-1]
        selected = (offsets >> bit_index & 1)[:, None] == 1
        moved = jnp.where(selected, moved[:, step_size:], moved[:, : cols - step_size])
    return moved


def picked(table, index):
    hit = index[:, None] == jnp.arange(table.shape[0], dtype=jnp.int32)[None, :]
    return jnp.sum(jnp.where(hit, table[None, :], 0), axis=1)


def delay_plan(sub_dev, held, tm_bits, freq_bits, shared, all_trials, choice_bits):
    terms = 1 + tm_bits + freq_bits
    local_bits = sub_dev.bit_length() - 1
    held_bits = held.bit_length() - 1

    def held_trial(m, right):
        value = np.zeros(terms, np.int64)
        for p in range(held_bits + tm_bits):
            if p < right:
                continue
            if p < held_bits:
                value[0] += (m >> p & 1) << (p - right)
            else:
                value[1 + p - held_bits] += 1 << (p - right)
        return value

    ids, rates, jits = [], [], []
    slot = {}
    for k in range(1, local_bits + 1):
        trial_count = 2**k
        for m in range(held):
            trial = held_trial(m, local_bits - k)
            for g in range(sub_dev >> k):
                key = (k, g, tuple(trial))
                if key in slot:
                    continue
                slot[key] = len(ids)
                rate = np.zeros(terms, np.int64)
                rate[0] = all_trials // trial_count - 1 + g
                for bit in range(freq_bits):
                    rate[1 + tm_bits + bit] = (sub_dev >> k) << bit
                jit = trial.copy()
                jit[0] += trial_count - 2
                ids.append(trial)
                rates.append(rate)
                jits.append(jit)
    paths = np.zeros((held * sub_dev, len(ids)), np.float32)
    for m in range(held):
        for i in range(sub_dev):
            for k in range(1, local_bits + 1):
                if i >> (k - 1) & 1:
                    key = (k, i >> k, tuple(held_trial(m, local_bits - k)))
                    paths[m * sub_dev + i, slot[key]] += 1.0
    unique_count = len(ids)
    level_rows = []
    now = np.zeros((held, terms), np.int64)
    for m in range(held):
        now[m] = held_trial(m, 0)
    for bit_index in range(freq_bits):
        trial_count = sub_dev * 2 ** (bit_index + 1)
        if bit_index >= freq_bits - shared:
            now = 2 * np.repeat(now, 2, axis=0)
            now[:, 0] = now[:, 0] + np.tile(np.arange(2), now.shape[0] // 2)
        else:
            now = 2 * now
            now[:, 1 + tm_bits + bit_index] = now[:, 1 + tm_bits + bit_index] + 1
        rate = np.zeros(terms, np.int64)
        rate[0] = all_trials // trial_count - 1
        for bit in range(bit_index + 1, freq_bits):
            rate[1 + tm_bits + bit] = 1 << (bit - bit_index - 1)
        choices = []
        spread_bits = choice_bits.get(bit_index, 0)
        for value in range(2**spread_bits):
            one = rate.copy()
            for step in range(spread_bits):
                one[1 + tm_bits + bit_index + 1 + step] = 0
            one[0] += value
            choices.append(one)
        for one in choices:
            for row in now:
                jit = row.copy()
                jit[0] += trial_count - 2
                ids.append(row.copy())
                rates.append(one)
                jits.append(jit)
        level_rows.append(now.shape[0] * len(choices))
    pack = lambda parts: np.stack(parts, axis=1).astype(np.int32)
    return pack(ids), pack(rates), pack(jits), paths, unique_count, level_rows


def shards(freq_axis, spectrogram, low_share, jitter):
    sub_dev = spectrogram.shape[0] // SUMMED
    span_time = spectrogram.shape[1]
    all_trials = low_share.shape[0] + 1
    freq_bits = lax.axis_size(freq_axis).bit_length() - 1
    tm_count = lax.axis_size("tm")
    shared = min(SHARED_LEVELS, freq_bits)
    device = lax.axis_index(freq_axis)
    place = lax.axis_index("tm")
    held = sub_dev // tm_count

    tm_bits = tm_count.bit_length() - 1
    groups = {}
    for first, names in ((1, ("zh", "zl")), (4, ("yl",))):
        width = sum(FINE_BITS[name] for name in names)
        redundant = {first + step >= freq_bits - shared for step in range(width)}
        if all(name in freq_axis for name in names) and len(redundant) == 1:
            groups[first] = (names, width)
    choice_bits = {}
    for first, (names, width) in groups.items():
        for step in range(width):
            choice_bits[first + step] = width - 1 - step
    id_terms, rate_terms, jitter_terms, paths, unique_count, level_rows = delay_plan(
        sub_dev, held, tm_bits, freq_bits, shared, all_trials, choice_bits
    )
    factors = jnp.concatenate(
        [jnp.ones((1,), jnp.int32),
         (place >> jnp.arange(tm_bits, dtype=jnp.int32) & 1).astype(jnp.int32),
         (device >> jnp.arange(freq_bits, dtype=jnp.int32) & 1).astype(jnp.int32)]
    )[:, None]
    ids_all = jnp.sum(factors * id_terms, axis=0)
    rates = picked(low_share, jnp.sum(factors * rate_terms, axis=0))
    jitters = picked(jitter, jnp.sum(factors * jitter_terms, axis=0))
    shift_table = (ids_all * rates + jitters) // 64
    path_shift = jnp.dot(
        paths, shift_table[:unique_count].astype(jnp.float32), precision=lax.Precision.HIGHEST
    )
    path_shift = jnp.round(path_shift).astype(jnp.int32)
    level_shifts = []
    start = unique_count
    for rows in level_rows:
        level_shifts.append(shift_table[start : start + rows])
        start = start + rows

    base = jnp.sum(spectrogram.reshape(sub_dev, SUMMED, span_time), axis=1, dtype=jnp.float32)
    spread = jnp.broadcast_to(base[None], (tm_count,) + base.shape)
    gathered = lax.all_to_all(spread, "tm", 0, 0, tiled=True)
    base = jnp.transpose(gathered, (1, 0, 2)).reshape(sub_dev, tm_count * span_time)
    full_time = base.shape[1]
    local_limit = sum(2**k - 1 for k in range(1, sub_dev.bit_length()))
    moved = shift_rows(jnp.tile(base, (held, 1)), path_shift, max(local_limit.bit_length(), 1))
    trial_rows = jnp.sum(moved.reshape(held, sub_dev, full_time), axis=1)
    level = 0
    for bit_index in range(freq_bits):
        need_now = sub_dev * 2 ** (bit_index + 1) - 1
        if bit_index in groups:
            names, width = groups[bit_index]
            spread = jnp.broadcast_to(trial_rows[None], (2**width,) + trial_rows.shape)
            peers = lax.all_to_all(spread, names, 0, 0, tiled=True)
            sets = [peers[index] for index in range(2**width)]
            for step in range(width):
                need_now = sub_dev * 2 ** (bit_index + step + 1) - 1
                if bit_index + step >= freq_bits - shared:
                    sets = [jnp.repeat(one, 2, axis=0) for one in sets]
                rows = sets[0].shape[0]
                merged = merge_rows(
                    jnp.concatenate(sets[0::2], axis=0),
                    zero_front(jnp.concatenate(sets[1::2], axis=0), need_now),
                    level_shifts[level],
                    need_now,
                )
                sets = [merged[index * rows : (index + 1) * rows] for index in range(len(sets) // 2)]
                level = level + 1
            trial_rows = sets[0]
            continue
        if any(0 < bit_index - first < groups[first][1] for first in groups):
            continue
        if bit_index == freq_bits - 1 and shared >= 3 and bit_index >= 2:
            partner = paired(trial_rows, freq_axis, near_half(bit_index, bit_index - 2))
        else:
            partner = swapped(trial_rows, freq_axis, bit_index)
        upper_half = device >> bit_index & 1
        low_rows = jnp.where(upper_half == 1, partner, trial_rows)
        high_rows = jnp.where(upper_half == 1, trial_rows, partner)
        if bit_index >= freq_bits - shared:
            low_rows = jnp.repeat(low_rows, 2, axis=0)
            high_rows = jnp.repeat(high_rows, 2, axis=0)
        trial_rows = merge_rows(
            low_rows, zero_front(high_rows, need_now), level_shifts[level], need_now
        )
        level = level + 1
    signal = trial_rows / math.sqrt(all_trials * SUMMED)
    peak_rows = []
    window_sum = signal
    width_now = 1
    for level_index in range(WIDTHS):
        peak_rows.append(jnp.max(window_sum, axis=0) / math.sqrt(width_now))
        if level_index + 1 < WIDTHS:
            window_sum = window_sum + zero_front(window_sum, width_now)[:, :full_time]
            width_now = width_now * 2
    best = jnp.stack(peak_rows).reshape(WIDTHS, tm_count, span_time)
    best = jnp.max(lax.all_to_all(best, "tm", 1, 1, tiled=True), axis=1)
    for bit_index in range(freq_bits - shared):
        if bit_index == 1 and "zl" in freq_axis and freq_bits - shared >= 4:
            spread = jnp.broadcast_to(best[None], (8,) + best.shape)
            best = jnp.max(lax.all_to_all(spread, ("zh", "zl"), 0, 0, tiled=True), axis=0)
        elif bit_index in (2, 3) and "zl" in freq_axis and freq_bits - shared >= 4:
            continue
        elif bit_index == 1 and "zl" in freq_axis:
            spread = jnp.broadcast_to(best[None], (4,) + best.shape)
            best = jnp.max(lax.all_to_all(spread, "zl", 0, 0, tiled=True), axis=0)
        elif bit_index == 2 and "zl" in freq_axis:
            continue
        elif bit_index == 3:
            best = jnp.maximum(best, paired(best, freq_axis, near_half(bit_index, 1)))
        else:
            best = jnp.maximum(best, swapped(best, freq_axis, bit_index))
    return best


def solution(mesh):
    count = mesh.shape["freq"]
    if count == 128:
        freq_axis, sizes = ("yh", "yl", "zh", "zl", "fc"), (2, 4, 2, 4, 2)
    elif count == 16:
        freq_axis, sizes = ("zh", "zl", "fc"), (2, 4, 2)
    else:
        freq_axis, sizes = ("freq",), (count,)
    fine = jax.sharding.Mesh(
        mesh.devices.reshape(sizes + (mesh.shape["tm"],)), freq_axis + ("tm",)
    )
    placed = (P(freq_axis, "tm"), P(), P())
    return jax.shard_map(
        functools.partial(shards, freq_axis), mesh=fine, in_specs=placed,
        out_specs=P(None, "tm"), check_vma=False,
    )
```

```python
import functools
import math

import numpy as np
import jax
import jax.numpy as jnp
from jax import lax
from jax.sharding import PartitionSpec as P

SUMMED = 32
WIDTHS = 9
SHARED_LEVELS = 3
NEAR_HALF = (6, 7, 4, 5, 2, 3, 0, 1)
FINE_BITS = {"yh": 1, "yl": 2, "zh": 1, "zl": 2, "fc": 1}


def swapped(block, axis, apart):
    count = lax.axis_size(axis)
    route = []
    for low in range(count):
        high = low | 1 << apart
        if high != low and high < count:
            route += [(low, high), (high, low)]
    return lax.ppermute(block, axis, route)


def paired(block, axis, partner_of):
    return lax.ppermute(block, axis, [(partner_of(i), i) for i in range(lax.axis_size(axis))])


def near_half(bit_index, ring_bits):
    def partner_of(i):
        ring = i >> ring_bits & 7
        return i - (ring << ring_bits) + (NEAR_HALF[ring] << ring_bits)

    return partner_of


def zero_front(rows, width):
    return jnp.pad(rows, [(0, 0)] * (rows.ndim - 1) + [(width, 0)])


def merge_rows(low_rows, high_rows, shifts, need_now):
    offsets = need_now - shifts
    bit_count = max(need_now.bit_length(), 1)
    moved = high_rows
    for bit_index in range(bit_count):
        step_size = 2**bit_index
        cols = moved.shape[-1]
        selected = (offsets >> bit_index & 1)[:, None] == 1
        moved = jnp.where(selected, moved[:, step_size:], moved[:, : cols - step_size])
    return low_rows + moved


def shift_rows(rows, shifts, bit_count):
    limit = 2**bit_count - 1
    offsets = limit - shifts
    moved = zero_front(rows, limit)
    for bit_index in range(bit_count):
        step_size = 2**bit_index
        cols = moved.shape[-1]
        selected = (offsets >> bit_index & 1)[:, None] == 1
        moved = jnp.where(selected, moved[:, step_size:], moved[:, : cols - step_size])
    return moved


def picked(table, index):
    hit = index[:, None] == jnp.arange(table.shape[0], dtype=jnp.int32)[None, :]
    return jnp.sum(jnp.where(hit, table[None, :], 0), axis=1)


def delay_plan(sub_dev, held, tm_bits, freq_bits, shared, all_trials, choice_bits):
    terms = 1 + tm_bits + freq_bits
    local_bits = sub_dev.bit_length() - 1
    held_bits = held.bit_length() - 1

    def held_trial(m, right):
        value = np.zeros(terms, np.int64)
        for p in range(held_bits + tm_bits):
            if p < right:
                continue
            if p < held_bits:
                value[0] += (m >> p & 1) << (p - right)
            else:
                value[1 + p - held_bits] += 1 << (p - right)
        return value

    ids, rates, jits = [], [], []
    slot = {}
    for k in range(1, local_bits + 1):
        trial_count = 2**k
        for m in range(held):
            trial = held_trial(m, local_bits - k)
            for g in range(sub_dev >> k):
                key = (k, g, tuple(trial))
                if key in slot:
                    continue
                slot[key] = len(ids)
                rate = np.zeros(terms, np.int64)
                rate[0] = all_trials // trial_count - 1 + g
                for bit in range(freq_bits):
                    rate[1 + tm_bits + bit] = (sub_dev >> k) << bit
                jit = trial.copy()
                jit[0] += trial_count - 2
                ids.append(trial)
                rates.append(rate)
                jits.append(jit)
    paths = np.zeros((held * sub_dev, len(ids)), np.float32)
    for m in range(held):
        for i in range(sub_dev):
            for k in range(1, local_bits + 1):
                if i >> (k - 1) & 1:
                    key = (k, i >> k, tuple(held_trial(m, local_bits - k)))
                    paths[m * sub_dev + i, slot[key]] += 1.0
    unique_count = len(ids)
    level_rows = []
    now = np.zeros((held, terms), np.int64)
    for m in range(held):
        now[m] = held_trial(m, 0)
    for bit_index in range(freq_bits):
        trial_count = sub_dev * 2 ** (bit_index + 1)
        if bit_index >= freq_bits - shared:
            now = 2 * np.repeat(now, 2, axis=0)
            now[:, 0] = now[:, 0] + np.tile(np.arange(2), now.shape[0] // 2)
        else:
            now = 2 * now
            now[:, 1 + tm_bits + bit_index] = now[:, 1 + tm_bits + bit_index] + 1
        rate = np.zeros(terms, np.int64)
        rate[0] = all_trials // trial_count - 1
        for bit in range(bit_index + 1, freq_bits):
            rate[1 + tm_bits + bit] = 1 << (bit - bit_index - 1)
        choices = []
        spread_bits = choice_bits.get(bit_index, 0)
        for value in range(2**spread_bits):
            one = rate.copy()
            for step in range(spread_bits):
                one[1 + tm_bits + bit_index + 1 + step] = 0
            one[0] += value
            choices.append(one)
        for one in choices:
            for row in now:
                jit = row.copy()
                jit[0] += trial_count - 2
                ids.append(row.copy())
                rates.append(one)
                jits.append(jit)
        level_rows.append(now.shape[0] * len(choices))
    pack = lambda parts: np.stack(parts, axis=1).astype(np.int32)
    return pack(ids), pack(rates), pack(jits), paths, unique_count, level_rows


def shards(freq_axis, spectrogram, low_share, jitter):
    sub_dev = spectrogram.shape[0] // SUMMED
    span_time = spectrogram.shape[1]
    all_trials = low_share.shape[0] + 1
    freq_bits = lax.axis_size(freq_axis).bit_length() - 1
    tm_count = lax.axis_size("tm")
    shared = min(SHARED_LEVELS, freq_bits)
    device = lax.axis_index(freq_axis)
    place = lax.axis_index("tm")
    held = sub_dev // tm_count

    tm_bits = tm_count.bit_length() - 1
    groups = {}
    for first, names in ((1, ("zh", "zl")), (4, ("yh", "yl"))):
        width = sum(FINE_BITS[name] for name in names)
        redundant = {first + step >= freq_bits - shared for step in range(width)}
        if all(name in freq_axis for name in names) and len(redundant) == 1:
            groups[first] = (names, width)
    choice_bits = {}
    for first, (names, width) in groups.items():
        for step in range(width):
            choice_bits[first + step] = width - 1 - step
    id_terms, rate_terms, jitter_terms, paths, unique_count, level_rows = delay_plan(
        sub_dev, held, tm_bits, freq_bits, shared, all_trials, choice_bits
    )
    factors = jnp.concatenate(
        [jnp.ones((1,), jnp.int32),
         (place >> jnp.arange(tm_bits, dtype=jnp.int32) & 1).astype(jnp.int32),
         (device >> jnp.arange(freq_bits, dtype=jnp.int32) & 1).astype(jnp.int32)]
    )[:, None]
    ids_all = jnp.sum(factors * id_terms, axis=0)
    rates = picked(low_share, jnp.sum(factors * rate_terms, axis=0))
    jitters = picked(jitter, jnp.sum(factors * jitter_terms, axis=0))
    shift_table = (ids_all * rates + jitters) // 64
    path_shift = jnp.dot(
        paths, shift_table[:unique_count].astype(jnp.float32), precision=lax.Precision.HIGHEST
    )
    path_shift = jnp.round(path_shift).astype(jnp.int32)
    level_shifts = []
    start = unique_count
    for rows in level_rows:
        level_shifts.append(shift_table[start : start + rows])
        start = start + rows

    base = jnp.sum(spectrogram.reshape(sub_dev, SUMMED, span_time), axis=1, dtype=jnp.float32)
    spread = jnp.broadcast_to(base[None], (tm_count,) + base.shape)
    gathered = lax.all_to_all(spread, "tm", 0, 0, tiled=True)
    base = jnp.transpose(gathered, (1, 0, 2)).reshape(sub_dev, tm_count * span_time)
    full_time = base.shape[1]
    local_limit = sum(2**k - 1 for k in range(1, sub_dev.bit_length()))
    moved = shift_rows(jnp.tile(base, (held, 1)), path_shift, max(local_limit.bit_length(), 1))
    trial_rows = jnp.sum(moved.reshape(held, sub_dev, full_time), axis=1)
    level = 0
    for bit_index in range(freq_bits):
        need_now = sub_dev * 2 ** (bit_index + 1) - 1
        if bit_index in groups:
            names, width = groups[bit_index]
            spread = jnp.broadcast_to(trial_rows[None], (2**width,) + trial_rows.shape)
            peers = lax.all_to_all(spread, names, 0, 0, tiled=True)
            sets = [peers[index] for index in range(2**width)]
            for step in range(width):
                need_now = sub_dev * 2 ** (bit_index + step + 1) - 1
                if bit_index + step >= freq_bits - shared:
                    sets = [jnp.repeat(one, 2, axis=0) for one in sets]
                rows = sets[0].shape[0]
                merged = merge_rows(
                    jnp.concatenate(sets[0::2], axis=0),
                    zero_front(jnp.concatenate(sets[1::2], axis=0), need_now),
                    level_shifts[level],
                    need_now,
                )
                sets = [merged[index * rows : (index + 1) * rows] for index in range(len(sets) // 2)]
                level = level + 1
            trial_rows = sets[0]
            continue
        if any(0 < bit_index - first < groups[first][1] for first in groups):
            continue
        if bit_index == freq_bits - 1 and shared >= 3 and bit_index >= 2:
            partner = paired(trial_rows, freq_axis, near_half(bit_index, bit_index - 2))
        else:
            partner = swapped(trial_rows, freq_axis, bit_index)
        upper_half = device >> bit_index & 1
        low_rows = jnp.where(upper_half == 1, partner, trial_rows)
        high_rows = jnp.where(upper_half == 1, trial_rows, partner)
        if bit_index >= freq_bits - shared:
            low_rows = jnp.repeat(low_rows, 2, axis=0)
            high_rows = jnp.repeat(high_rows, 2, axis=0)
        trial_rows = merge_rows(
            low_rows, zero_front(high_rows, need_now), level_shifts[level], need_now
        )
        level = level + 1
    signal = trial_rows / math.sqrt(all_trials * SUMMED)
    peak_rows = []
    window_sum = signal
    width_now = 1
    for level_index in range(WIDTHS):
        peak_rows.append(jnp.max(window_sum, axis=0) / math.sqrt(width_now))
        if level_index + 1 < WIDTHS:
            window_sum = window_sum + zero_front(window_sum, width_now)[:, :full_time]
            width_now = width_now * 2
    best = jnp.stack(peak_rows).reshape(WIDTHS, tm_count, span_time)
    best = jnp.max(lax.all_to_all(best, "tm", 1, 1, tiled=True), axis=1)
    for bit_index in range(freq_bits - shared):
        if bit_index == 1 and "zl" in freq_axis and freq_bits - shared >= 4:
            spread = jnp.broadcast_to(best[None], (8,) + best.shape)
            best = jnp.max(lax.all_to_all(spread, ("zh", "zl"), 0, 0, tiled=True), axis=0)
        elif bit_index in (2, 3) and "zl" in freq_axis and freq_bits - shared >= 4:
            continue
        elif bit_index == 1 and "zl" in freq_axis:
            spread = jnp.broadcast_to(best[None], (4,) + best.shape)
            best = jnp.max(lax.all_to_all(spread, "zl", 0, 0, tiled=True), axis=0)
        elif bit_index == 2 and "zl" in freq_axis:
            continue
        elif bit_index == 3:
            best = jnp.maximum(best, paired(best, freq_axis, near_half(bit_index, 1)))
        else:
            best = jnp.maximum(best, swapped(best, freq_axis, bit_index))
    return best


def solution(mesh):
    count = mesh.shape["freq"]
    if count == 128:
        freq_axis, sizes = ("yh", "yl", "zh", "zl", "fc"), (2, 4, 2, 4, 2)
    elif count == 16:
        freq_axis, sizes = ("zh", "zl", "fc"), (2, 4, 2)
    else:
        freq_axis, sizes = ("freq",), (count,)
    fine = jax.sharding.Mesh(
        mesh.devices.reshape(sizes + (mesh.shape["tm"],)), freq_axis + ("tm",)
    )
    placed = (P(freq_axis, "tm"), P(), P())
    return jax.shard_map(
        functools.partial(shards, freq_axis), mesh=fine, in_specs=placed,
        out_specs=P(None, "tm"), check_vma=False,
    )
```

```python
import functools
import math

import numpy as np
import jax
import jax.numpy as jnp
from jax import lax
from jax.sharding import PartitionSpec as P

SUMMED = 32
WIDTHS = 9
SHARED_LEVELS = 3
NEAR_HALF = (6, 7, 4, 5, 2, 3, 0, 1)
FINE_BITS = {"yh": 1, "yl": 2, "zh": 1, "zl": 2, "fc": 1}


def swapped(block, axis, apart):
    count = lax.axis_size(axis)
    route = []
    for low in range(count):
        high = low | 1 << apart
        if high != low and high < count:
            route += [(low, high), (high, low)]
    return lax.ppermute(block, axis, route)


def paired(block, axis, partner_of):
    return lax.ppermute(block, axis, [(partner_of(i), i) for i in range(lax.axis_size(axis))])


def near_half(bit_index, ring_bits):
    def partner_of(i):
        ring = i >> ring_bits & 7
        return i - (ring << ring_bits) + (NEAR_HALF[ring] << ring_bits)

    return partner_of


def zero_front(rows, width):
    return jnp.pad(rows, [(0, 0)] * (rows.ndim - 1) + [(width, 0)])


def merge_rows(low_rows, high_rows, shifts, need_now):
    offsets = need_now - shifts
    bit_count = max(need_now.bit_length(), 1)
    moved = high_rows
    for bit_index in range(bit_count):
        step_size = 2**bit_index
        cols = moved.shape[-1]
        selected = (offsets >> bit_index & 1)[:, None] == 1
        moved = jnp.where(selected, moved[:, step_size:], moved[:, : cols - step_size])
    return low_rows + moved


def shift_rows(rows, shifts, bit_count):
    limit = 2**bit_count - 1
    offsets = limit - shifts
    moved = zero_front(rows, limit)
    for bit_index in range(bit_count):
        step_size = 2**bit_index
        cols = moved.shape[-1]
        selected = (offsets >> bit_index & 1)[:, None] == 1
        moved = jnp.where(selected, moved[:, step_size:], moved[:, : cols - step_size])
    return moved


def picked(table, index):
    hit = index[:, None] == jnp.arange(table.shape[0], dtype=jnp.int32)[None, :]
    return jnp.sum(jnp.where(hit, table[None, :], 0), axis=1)


def delay_plan(sub_dev, held, tm_bits, freq_bits, shared, all_trials, choice_bits):
    terms = 1 + tm_bits + freq_bits
    local_bits = sub_dev.bit_length() - 1
    held_bits = held.bit_length() - 1

    def held_trial(m, right):
        value = np.zeros(terms, np.int64)
        for p in range(held_bits + tm_bits):
            if p < right:
                continue
            if p < held_bits:
                value[0] += (m >> p & 1) << (p - right)
            else:
                value[1 + p - held_bits] += 1 << (p - right)
        return value

    ids, rates, jits = [], [], []
    slot = {}
    for k in range(1, local_bits + 1):
        trial_count = 2**k
        for m in range(held):
            trial = held_trial(m, local_bits - k)
            for g in range(sub_dev >> k):
                key = (k, g, tuple(trial))
                if key in slot:
                    continue
                slot[key] = len(ids)
                rate = np.zeros(terms, np.int64)
                rate[0] = all_trials // trial_count - 1 + g
                for bit in range(freq_bits):
                    rate[1 + tm_bits + bit] = (sub_dev >> k) << bit
                jit = trial.copy()
                jit[0] += trial_count - 2
                ids.append(trial)
                rates.append(rate)
                jits.append(jit)
    paths = np.zeros((held * sub_dev, len(ids)), np.float32)
    for m in range(held):
        for i in range(sub_dev):
            for k in range(1, local_bits + 1):
                if i >> (k - 1) & 1:
                    key = (k, i >> k, tuple(held_trial(m, local_bits - k)))
                    paths[m * sub_dev + i, slot[key]] += 1.0
    unique_count = len(ids)
    level_rows = []
    now = np.zeros((held, terms), np.int64)
    for m in range(held):
        now[m] = held_trial(m, 0)
    for bit_index in range(freq_bits):
        trial_count = sub_dev * 2 ** (bit_index + 1)
        if bit_index >= freq_bits - shared:
            now = 2 * np.repeat(now, 2, axis=0)
            now[:, 0] = now[:, 0] + np.tile(np.arange(2), now.shape[0] // 2)
        else:
            now = 2 * now
            now[:, 1 + tm_bits + bit_index] = now[:, 1 + tm_bits + bit_index] + 1
        rate = np.zeros(terms, np.int64)
        rate[0] = all_trials // trial_count - 1
        for bit in range(bit_index + 1, freq_bits):
            rate[1 + tm_bits + bit] = 1 << (bit - bit_index - 1)
        choices = []
        spread_bits = choice_bits.get(bit_index, 0)
        for value in range(2**spread_bits):
            one = rate.copy()
            for step in range(spread_bits):
                one[1 + tm_bits + bit_index + 1 + step] = 0
            one[0] += value
            choices.append(one)
        for one in choices:
            for row in now:
                jit = row.copy()
                jit[0] += trial_count - 2
                ids.append(row.copy())
                rates.append(one)
                jits.append(jit)
        level_rows.append(now.shape[0] * len(choices))
    pack = lambda parts: np.stack(parts, axis=1).astype(np.int32)
    return pack(ids), pack(rates), pack(jits), paths, unique_count, level_rows


def shards(freq_axis, spectrogram, low_share, jitter):
    sub_dev = spectrogram.shape[0] // SUMMED
    span_time = spectrogram.shape[1]
    all_trials = low_share.shape[0] + 1
    freq_bits = lax.axis_size(freq_axis).bit_length() - 1
    tm_count = lax.axis_size("tm")
    shared = min(SHARED_LEVELS, freq_bits)
    device = lax.axis_index(freq_axis)
    place = lax.axis_index("tm")
    held = sub_dev // tm_count

    tm_bits = tm_count.bit_length() - 1
    groups = {}
    for first, names in ((1, ("zh", "zl")), (4, ("yl",))):
        width = sum(FINE_BITS[name] for name in names)
        redundant = {first + step >= freq_bits - shared for step in range(width)}
        if all(name in freq_axis for name in names) and len(redundant) == 1:
            groups[first] = (names, width)
    choice_bits = {}
    for first, (names, width) in groups.items():
        for step in range(width):
            choice_bits[first + step] = width - 1 - step
    id_terms, rate_terms, jitter_terms, paths, unique_count, level_rows = delay_plan(
        sub_dev, held, tm_bits, freq_bits, shared, all_trials, choice_bits
    )
    factors = jnp.concatenate(
        [jnp.ones((1,), jnp.int32),
         (place >> jnp.arange(tm_bits, dtype=jnp.int32) & 1).astype(jnp.int32),
         (device >> jnp.arange(freq_bits, dtype=jnp.int32) & 1).astype(jnp.int32)]
    )[:, None]
    ids_all = jnp.sum(factors * id_terms, axis=0)
    rates = picked(low_share, jnp.sum(factors * rate_terms, axis=0))
    jitters = picked(jitter, jnp.sum(factors * jitter_terms, axis=0))
    shift_table = (ids_all * rates + jitters) // 64
    path_shift = jnp.dot(
        paths, shift_table[:unique_count].astype(jnp.float32), precision=lax.Precision.HIGHEST
    )
    path_shift = jnp.round(path_shift).astype(jnp.int32)
    level_shifts = []
    start = unique_count
    for rows in level_rows:
        level_shifts.append(shift_table[start : start + rows])
        start = start + rows

    base = jnp.sum(spectrogram.reshape(sub_dev, SUMMED, span_time), axis=1, dtype=jnp.float32)
    spread = jnp.broadcast_to(base[None], (tm_count,) + base.shape)
    gathered = lax.all_to_all(spread, "tm", 0, 0, tiled=True)
    base = jnp.transpose(gathered, (1, 0, 2)).reshape(sub_dev, tm_count * span_time)
    full_time = base.shape[1]
    local_limit = sum(2**k - 1 for k in range(1, sub_dev.bit_length()))
    moved = shift_rows(jnp.tile(base, (held, 1)), path_shift, max(local_limit.bit_length(), 1))
    trial_rows = jnp.sum(moved.reshape(held, sub_dev, full_time), axis=1)
    level = 0
    for bit_index in range(freq_bits):
        need_now = sub_dev * 2 ** (bit_index + 1) - 1
        if bit_index in groups:
            names, width = groups[bit_index]
            spread = jnp.broadcast_to(trial_rows[None], (2**width,) + trial_rows.shape)
            peers = lax.all_to_all(spread, names, 0, 0, tiled=True)
            sets = [peers[index] for index in range(2**width)]
            for step in range(width):
                need_now = sub_dev * 2 ** (bit_index + step + 1) - 1
                if bit_index + step >= freq_bits - shared:
                    sets = [jnp.repeat(one, 2, axis=0) for one in sets]
                rows = sets[0].shape[0]
                merged = merge_rows(
                    jnp.concatenate(sets[0::2], axis=0),
                    zero_front(jnp.concatenate(sets[1::2], axis=0), need_now),
                    level_shifts[level],
                    need_now,
                )
                sets = [merged[index * rows : (index + 1) * rows] for index in range(len(sets) // 2)]
                level = level + 1
            trial_rows = sets[0]
            continue
        if any(0 < bit_index - first < groups[first][1] for first in groups):
            continue
        if bit_index == freq_bits - 1 and shared >= 3 and bit_index >= 2:
            partner = paired(trial_rows, freq_axis, near_half(bit_index, bit_index - 2))
        else:
            partner = swapped(trial_rows, freq_axis, bit_index)
        upper_half = device >> bit_index & 1
        low_rows = jnp.where(upper_half == 1, partner, trial_rows)
        high_rows = jnp.where(upper_half == 1, trial_rows, partner)
        if bit_index >= freq_bits - shared:
            low_rows = jnp.repeat(low_rows, 2, axis=0)
            high_rows = jnp.repeat(high_rows, 2, axis=0)
        trial_rows = merge_rows(
            low_rows, zero_front(high_rows, need_now), level_shifts[level], need_now
        )
        level = level + 1
    signal = trial_rows / math.sqrt(all_trials * SUMMED)
    peak_rows = []
    window_sum = signal
    width_now = 1
    for level_index in range(WIDTHS):
        peak_rows.append(jnp.max(window_sum, axis=0) / math.sqrt(width_now))
        if level_index + 1 < WIDTHS:
            window_sum = window_sum + zero_front(window_sum, width_now)[:, :full_time]
            width_now = width_now * 2
    best = jnp.stack(peak_rows).reshape(WIDTHS, tm_count, span_time)
    joint = "zl" in freq_axis and freq_bits - shared >= 4
    if joint:
        blocks = jnp.transpose(best, (1, 0, 2))
        spread = jnp.broadcast_to(blocks[None], (8,) + blocks.shape).reshape((-1,) + blocks.shape[1:])
        best = jnp.max(lax.all_to_all(spread, ("zh", "zl", "tm"), 0, 0, tiled=True), axis=0)
    else:
        best = jnp.max(lax.all_to_all(best, "tm", 1, 1, tiled=True), axis=1)
    for bit_index in range(freq_bits - shared):
        if bit_index in (1, 2, 3) and joint:
            continue
        elif bit_index == 1 and "zl" in freq_axis:
            spread = jnp.broadcast_to(best[None], (4,) + best.shape)
            best = jnp.max(lax.all_to_all(spread, "zl", 0, 0, tiled=True), axis=0)
        elif bit_index == 2 and "zl" in freq_axis:
            continue
        elif bit_index == 3:
            best = jnp.maximum(best, paired(best, freq_axis, near_half(bit_index, 1)))
        else:
            best = jnp.maximum(best, swapped(best, freq_axis, bit_index))
    return best


def solution(mesh):
    count = mesh.shape["freq"]
    if count == 128:
        freq_axis, sizes = ("yh", "yl", "zh", "zl", "fc"), (2, 4, 2, 4, 2)
    elif count == 16:
        freq_axis, sizes = ("zh", "zl", "fc"), (2, 4, 2)
    else:
        freq_axis, sizes = ("freq",), (count,)
    fine = jax.sharding.Mesh(
        mesh.devices.reshape(sizes + (mesh.shape["tm"],)), freq_axis + ("tm",)
    )
    placed = (P(freq_axis, "tm"), P(), P())
    return jax.shard_map(
        functools.partial(shards, freq_axis), mesh=fine, in_specs=placed,
        out_specs=P(None, "tm"), check_vma=False,
    )
```

```python
import functools
import math

import numpy as np
import jax
import jax.numpy as jnp
from jax import lax
from jax.sharding import PartitionSpec as P

SUMMED = 32
WIDTHS = 9
SHARED_LEVELS = 3
NEAR_HALF = (6, 7, 4, 5, 2, 3, 0, 1)
FINE_BITS = {"yh": 1, "yl": 2, "zh": 1, "zl": 2, "fc": 1}


def swapped(block, axis, apart):
    count = lax.axis_size(axis)
    route = []
    for low in range(count):
        high = low | 1 << apart
        if high != low and high < count:
            route += [(low, high), (high, low)]
    return lax.ppermute(block, axis, route)


def paired(block, axis, partner_of):
    return lax.ppermute(block, axis, [(partner_of(i), i) for i in range(lax.axis_size(axis))])


def near_half(bit_index, ring_bits):
    def partner_of(i):
        ring = i >> ring_bits & 7
        return i - (ring << ring_bits) + (NEAR_HALF[ring] << ring_bits)

    return partner_of


def zero_front(rows, width):
    return jnp.pad(rows, [(0, 0)] * (rows.ndim - 1) + [(width, 0)])


def merge_rows(low_rows, high_rows, shifts, need_now):
    offsets = need_now - shifts
    bit_count = max(need_now.bit_length(), 1)
    moved = high_rows
    for bit_index in range(bit_count):
        step_size = 2**bit_index
        cols = moved.shape[-1]
        selected = (offsets >> bit_index & 1)[:, None] == 1
        moved = jnp.where(selected, moved[:, step_size:], moved[:, : cols - step_size])
    return low_rows + moved


def shift_rows(rows, shifts, bit_count):
    limit = 2**bit_count - 1
    offsets = limit - shifts
    moved = zero_front(rows, limit)
    for bit_index in range(bit_count):
        step_size = 2**bit_index
        cols = moved.shape[-1]
        selected = (offsets >> bit_index & 1)[:, None] == 1
        moved = jnp.where(selected, moved[:, step_size:], moved[:, : cols - step_size])
    return moved


def picked(table, index):
    hit = index[:, None] == jnp.arange(table.shape[0], dtype=jnp.int32)[None, :]
    return jnp.sum(jnp.where(hit, table[None, :], 0), axis=1)


def delay_plan(sub_dev, held, tm_bits, freq_bits, shared, all_trials, choice_bits):
    terms = 1 + tm_bits + freq_bits
    local_bits = sub_dev.bit_length() - 1
    held_bits = held.bit_length() - 1

    def held_trial(m, right):
        value = np.zeros(terms, np.int64)
        for p in range(held_bits + tm_bits):
            if p < right:
                continue
            if p < held_bits:
                value[0] += (m >> p & 1) << (p - right)
            else:
                value[1 + p - held_bits] += 1 << (p - right)
        return value

    ids, rates, jits = [], [], []
    slot = {}
    for k in range(1, local_bits + 1):
        trial_count = 2**k
        for m in range(held):
            trial = held_trial(m, local_bits - k)
            for g in range(sub_dev >> k):
                key = (k, g, tuple(trial))
                if key in slot:
                    continue
                slot[key] = len(ids)
                rate = np.zeros(terms, np.int64)
                rate[0] = all_trials // trial_count - 1 + g
                for bit in range(freq_bits):
                    rate[1 + tm_bits + bit] = (sub_dev >> k) << bit
                jit = trial.copy()
                jit[0] += trial_count - 2
                ids.append(trial)
                rates.append(rate)
                jits.append(jit)
    paths = np.zeros((held * sub_dev, len(ids)), np.float32)
    for m in range(held):
        for i in range(sub_dev):
            for k in range(1, local_bits + 1):
                if i >> (k - 1) & 1:
                    key = (k, i >> k, tuple(held_trial(m, local_bits - k)))
                    paths[m * sub_dev + i, slot[key]] += 1.0
    unique_count = len(ids)
    level_rows = []
    now = np.zeros((held, terms), np.int64)
    for m in range(held):
        now[m] = held_trial(m, 0)
    for bit_index in range(freq_bits):
        trial_count = sub_dev * 2 ** (bit_index + 1)
        if bit_index >= freq_bits - shared:
            now = 2 * np.repeat(now, 2, axis=0)
            now[:, 0] = now[:, 0] + np.tile(np.arange(2), now.shape[0] // 2)
        else:
            now = 2 * now
            now[:, 1 + tm_bits + bit_index] = now[:, 1 + tm_bits + bit_index] + 1
        rate = np.zeros(terms, np.int64)
        rate[0] = all_trials // trial_count - 1
        for bit in range(bit_index + 1, freq_bits):
            rate[1 + tm_bits + bit] = 1 << (bit - bit_index - 1)
        choices = []
        spread_bits = choice_bits.get(bit_index, 0)
        for value in range(2**spread_bits):
            one = rate.copy()
            for step in range(spread_bits):
                one[1 + tm_bits + bit_index + 1 + step] = 0
            one[0] += value
            choices.append(one)
        for one in choices:
            for row in now:
                jit = row.copy()
                jit[0] += trial_count - 2
                ids.append(row.copy())
                rates.append(one)
                jits.append(jit)
        level_rows.append(now.shape[0] * len(choices))
    pack = lambda parts: np.stack(parts, axis=1).astype(np.int32)
    return pack(ids), pack(rates), pack(jits), paths, unique_count, level_rows


def shards(freq_axis, spectrogram, low_share, jitter):
    sub_dev = spectrogram.shape[0] // SUMMED
    span_time = spectrogram.shape[1]
    all_trials = low_share.shape[0] + 1
    freq_bits = lax.axis_size(freq_axis).bit_length() - 1
    tm_count = lax.axis_size("tm")
    shared = min(SHARED_LEVELS, freq_bits)
    device = lax.axis_index(freq_axis)
    place = lax.axis_index("tm")
    held = sub_dev // tm_count

    tm_bits = tm_count.bit_length() - 1
    groups = {}
    for first, names in ((1, ("zh", "zl")), (4, ("yl",))):
        width = sum(FINE_BITS[name] for name in names)
        redundant = {first + step >= freq_bits - shared for step in range(width)}
        if all(name in freq_axis for name in names) and len(redundant) == 1:
            groups[first] = (names, width)
    choice_bits = {}
    for first, (names, width) in groups.items():
        for step in range(width):
            choice_bits[first + step] = width - 1 - step
    id_terms, rate_terms, jitter_terms, paths, unique_count, level_rows = delay_plan(
        sub_dev, held, tm_bits, freq_bits, shared, all_trials, choice_bits
    )
    factors = jnp.concatenate(
        [jnp.ones((1,), jnp.int32),
         (place >> jnp.arange(tm_bits, dtype=jnp.int32) & 1).astype(jnp.int32),
         (device >> jnp.arange(freq_bits, dtype=jnp.int32) & 1).astype(jnp.int32)]
    )[:, None]
    ids_all = jnp.sum(factors * id_terms, axis=0)
    rates = picked(low_share, jnp.sum(factors * rate_terms, axis=0))
    jitters = picked(jitter, jnp.sum(factors * jitter_terms, axis=0))
    shift_table = (ids_all * rates + jitters) // 64
    path_shift = jnp.dot(
        paths, shift_table[:unique_count].astype(jnp.float32), precision=lax.Precision.HIGHEST
    )
    path_shift = jnp.round(path_shift).astype(jnp.int32)
    level_shifts = []
    start = unique_count
    for rows in level_rows:
        level_shifts.append(shift_table[start : start + rows])
        start = start + rows

    base = jnp.sum(spectrogram.reshape(sub_dev, SUMMED, span_time), axis=1, dtype=jnp.float32)
    spread = jnp.broadcast_to(base[None], (tm_count,) + base.shape)
    gathered = lax.all_to_all(spread, "tm", 0, 0, tiled=True)
    base = jnp.transpose(gathered, (1, 0, 2)).reshape(sub_dev, tm_count * span_time)
    full_time = base.shape[1]
    local_limit = sum(2**k - 1 for k in range(1, sub_dev.bit_length()))
    moved = shift_rows(jnp.tile(base, (held, 1)), path_shift, max(local_limit.bit_length(), 1))
    trial_rows = jnp.sum(moved.reshape(held, sub_dev, full_time), axis=1)
    level = 0
    for bit_index in range(freq_bits):
        need_now = sub_dev * 2 ** (bit_index + 1) - 1
        if bit_index in groups:
            names, width = groups[bit_index]
            spread = jnp.broadcast_to(trial_rows[None], (2**width,) + trial_rows.shape)
            peers = lax.all_to_all(spread, names, 0, 0, tiled=True)
            sets = [peers[index] for index in range(2**width)]
            for step in range(width):
                need_now = sub_dev * 2 ** (bit_index + step + 1) - 1
                if bit_index + step >= freq_bits - shared:
                    sets = [jnp.repeat(one, 2, axis=0) for one in sets]
                rows = sets[0].shape[0]
                merged = merge_rows(
                    jnp.concatenate(sets[0::2], axis=0),
                    zero_front(jnp.concatenate(sets[1::2], axis=0), need_now),
                    level_shifts[level],
                    need_now,
                )
                sets = [merged[index * rows : (index + 1) * rows] for index in range(len(sets) // 2)]
                level = level + 1
            trial_rows = sets[0]
            continue
        if any(0 < bit_index - first < groups[first][1] for first in groups):
            continue
        if bit_index == freq_bits - 1 and shared >= 3 and bit_index >= 2:
            partner = paired(trial_rows, freq_axis, near_half(bit_index, bit_index - 2))
        else:
            partner = swapped(trial_rows, freq_axis, bit_index)
        upper_half = device >> bit_index & 1
        low_rows = jnp.where(upper_half == 1, partner, trial_rows)
        high_rows = jnp.where(upper_half == 1, trial_rows, partner)
        if bit_index >= freq_bits - shared:
            low_rows = jnp.repeat(low_rows, 2, axis=0)
            high_rows = jnp.repeat(high_rows, 2, axis=0)
        trial_rows = merge_rows(
            low_rows, zero_front(high_rows, need_now), level_shifts[level], need_now
        )
        level = level + 1
    signal = trial_rows / math.sqrt(all_trials * SUMMED)
    peak_rows = []
    window_sum = signal
    width_now = 1
    for level_index in range(WIDTHS):
        peak_rows.append(jnp.max(window_sum, axis=0) / math.sqrt(width_now))
        if level_index + 1 < WIDTHS:
            window_sum = window_sum + zero_front(window_sum, width_now)[:, :full_time]
            width_now = width_now * 2
    best = jnp.stack(peak_rows).reshape(WIDTHS, tm_count, span_time)
    best = jnp.max(lax.all_to_all(best, "tm", 1, 1, tiled=True), axis=1)
    for bit_index in range(freq_bits - shared):
        if bit_index == 0 and "zl" in freq_axis and freq_bits - shared >= 4:
            spread = jnp.broadcast_to(best[None], (16,) + best.shape)
            best = jnp.max(lax.all_to_all(spread, ("zh", "zl", "fc"), 0, 0, tiled=True), axis=0)
        elif bit_index in (1, 2, 3) and "zl" in freq_axis and freq_bits - shared >= 4:
            continue
        elif bit_index == 1 and "zl" in freq_axis:
            spread = jnp.broadcast_to(best[None], (4,) + best.shape)
            best = jnp.max(lax.all_to_all(spread, "zl", 0, 0, tiled=True), axis=0)
        elif bit_index == 2 and "zl" in freq_axis:
            continue
        elif bit_index == 3:
            best = jnp.maximum(best, paired(best, freq_axis, near_half(bit_index, 1)))
        else:
            best = jnp.maximum(best, swapped(best, freq_axis, bit_index))
    return best


def solution(mesh):
    count = mesh.shape["freq"]
    if count == 128:
        freq_axis, sizes = ("yh", "yl", "zh", "zl", "fc"), (2, 4, 2, 4, 2)
    elif count == 16:
        freq_axis, sizes = ("zh", "zl", "fc"), (2, 4, 2)
    else:
        freq_axis, sizes = ("freq",), (count,)
    fine = jax.sharding.Mesh(
        mesh.devices.reshape(sizes + (mesh.shape["tm"],)), freq_axis + ("tm",)
    )
    placed = (P(freq_axis, "tm"), P(), P())
    return jax.shard_map(
        functools.partial(shards, freq_axis), mesh=fine, in_specs=placed,
        out_specs=P(None, "tm"), check_vma=False,
    )
```

```python
import functools
import math

import numpy as np
import jax
import jax.numpy as jnp
from jax import lax
from jax.sharding import PartitionSpec as P

SUMMED = 32
WIDTHS = 9
SHARED_LEVELS = 3
NEAR_HALF = (6, 7, 4, 5, 2, 3, 0, 1)
FINE_BITS = {"yh": 1, "yl": 2, "zh": 1, "zl": 2, "fc": 1}


def swapped(block, axis, apart):
    count = lax.axis_size(axis)
    route = []
    for low in range(count):
        high = low | 1 << apart
        if high != low and high < count:
            route += [(low, high), (high, low)]
    return lax.ppermute(block, axis, route)


def paired(block, axis, partner_of):
    return lax.ppermute(block, axis, [(partner_of(i), i) for i in range(lax.axis_size(axis))])


def near_half(bit_index, ring_bits):
    def partner_of(i):
        ring = i >> ring_bits & 7
        return i - (ring << ring_bits) + (NEAR_HALF[ring] << ring_bits)

    return partner_of


def zero_front(rows, width):
    return jnp.pad(rows, [(0, 0)] * (rows.ndim - 1) + [(width, 0)])


def merge_rows(low_rows, high_rows, shifts, need_now, copies=0):
    offsets = need_now - shifts
    bit_count = max(need_now.bit_length(), 1)
    moved = high_rows
    for bit_index in range(bit_count):
        step_size = 2**bit_index
        cols = moved.shape[-1]
        selected = (offsets >> bit_index & 1)[:, None] == 1
        moved = jnp.where(selected, moved[:, step_size:], moved[:, : cols - step_size])
    if copies:
        return jnp.broadcast_to(low_rows[None], (copies,) + low_rows.shape) + jnp.broadcast_to(
            moved[None], (copies,) + moved.shape
        )
    return low_rows + moved


def shift_rows(rows, shifts, bit_count):
    limit = 2**bit_count - 1
    offsets = limit - shifts
    moved = zero_front(rows, limit)
    for bit_index in range(bit_count):
        step_size = 2**bit_index
        cols = moved.shape[-1]
        selected = (offsets >> bit_index & 1)[:, None] == 1
        moved = jnp.where(selected, moved[:, step_size:], moved[:, : cols - step_size])
    return moved


def picked(table, index):
    hit = index[:, None] == jnp.arange(table.shape[0], dtype=jnp.int32)[None, :]
    return jnp.sum(jnp.where(hit, table[None, :], 0), axis=1)


def delay_plan(sub_dev, held, tm_bits, freq_bits, shared, all_trials, choice_bits):
    terms = 1 + tm_bits + freq_bits
    local_bits = sub_dev.bit_length() - 1
    held_bits = held.bit_length() - 1

    def held_trial(m, right):
        value = np.zeros(terms, np.int64)
        for p in range(held_bits + tm_bits):
            if p < right:
                continue
            if p < held_bits:
                value[0] += (m >> p & 1) << (p - right)
            else:
                value[1 + p - held_bits] += 1 << (p - right)
        return value

    ids, rates, jits = [], [], []
    slot = {}
    for k in range(1, local_bits + 1):
        trial_count = 2**k
        for m in range(held):
            trial = held_trial(m, local_bits - k)
            for g in range(sub_dev >> k):
                key = (k, g, tuple(trial))
                if key in slot:
                    continue
                slot[key] = len(ids)
                rate = np.zeros(terms, np.int64)
                rate[0] = all_trials // trial_count - 1 + g
                for bit in range(freq_bits):
                    rate[1 + tm_bits + bit] = (sub_dev >> k) << bit
                jit = trial.copy()
                jit[0] += trial_count - 2
                ids.append(trial)
                rates.append(rate)
                jits.append(jit)
    paths = np.zeros((held * sub_dev, len(ids)), np.float32)
    for m in range(held):
        for i in range(sub_dev):
            for k in range(1, local_bits + 1):
                if i >> (k - 1) & 1:
                    key = (k, i >> k, tuple(held_trial(m, local_bits - k)))
                    paths[m * sub_dev + i, slot[key]] += 1.0
    unique_count = len(ids)
    level_rows = []
    now = np.zeros((held, terms), np.int64)
    for m in range(held):
        now[m] = held_trial(m, 0)
    for bit_index in range(freq_bits):
        trial_count = sub_dev * 2 ** (bit_index + 1)
        if bit_index >= freq_bits - shared:
            now = 2 * np.repeat(now, 2, axis=0)
            now[:, 0] = now[:, 0] + np.tile(np.arange(2), now.shape[0] // 2)
        else:
            now = 2 * now
            now[:, 1 + tm_bits + bit_index] = now[:, 1 + tm_bits + bit_index] + 1
        rate = np.zeros(terms, np.int64)
        rate[0] = all_trials // trial_count - 1
        for bit in range(bit_index + 1, freq_bits):
            rate[1 + tm_bits + bit] = 1 << (bit - bit_index - 1)
        choices = []
        spread_bits = choice_bits.get(bit_index, 0)
        for value in range(2**spread_bits):
            one = rate.copy()
            for step in range(spread_bits):
                one[1 + tm_bits + bit_index + 1 + step] = 0
            one[0] += value
            choices.append(one)
        for one in choices:
            for row in now:
                jit = row.copy()
                jit[0] += trial_count - 2
                ids.append(row.copy())
                rates.append(one)
                jits.append(jit)
        level_rows.append(now.shape[0] * len(choices))
    pack = lambda parts: np.stack(parts, axis=1).astype(np.int32)
    return pack(ids), pack(rates), pack(jits), paths, unique_count, level_rows


def shards(freq_axis, spectrogram, low_share, jitter):
    sub_dev = spectrogram.shape[0] // SUMMED
    span_time = spectrogram.shape[1]
    all_trials = low_share.shape[0] + 1
    freq_bits = lax.axis_size(freq_axis).bit_length() - 1
    tm_count = lax.axis_size("tm")
    shared = min(SHARED_LEVELS, freq_bits)
    device = lax.axis_index(freq_axis)
    place = lax.axis_index("tm")
    held = sub_dev // tm_count

    tm_bits = tm_count.bit_length() - 1
    groups = {}
    for first, names in ((1, ("zh", "zl")), (4, ("yl",))):
        width = sum(FINE_BITS[name] for name in names)
        redundant = {first + step >= freq_bits - shared for step in range(width)}
        if all(name in freq_axis for name in names) and len(redundant) == 1:
            groups[first] = (names, width)
    choice_bits = {}
    for first, (names, width) in groups.items():
        for step in range(width):
            choice_bits[first + step] = width - 1 - step
    id_terms, rate_terms, jitter_terms, paths, unique_count, level_rows = delay_plan(
        sub_dev, held, tm_bits, freq_bits, shared, all_trials, choice_bits
    )
    factors = jnp.concatenate(
        [jnp.ones((1,), jnp.int32),
         (place >> jnp.arange(tm_bits, dtype=jnp.int32) & 1).astype(jnp.int32),
         (device >> jnp.arange(freq_bits, dtype=jnp.int32) & 1).astype(jnp.int32)]
    )[:, None]
    ids_all = jnp.sum(factors * id_terms, axis=0)
    rates = picked(low_share, jnp.sum(factors * rate_terms, axis=0))
    jitters = picked(jitter, jnp.sum(factors * jitter_terms, axis=0))
    shift_table = (ids_all * rates + jitters) // 64
    path_shift = jnp.dot(
        paths, shift_table[:unique_count].astype(jnp.float32), precision=lax.Precision.HIGHEST
    )
    path_shift = jnp.round(path_shift).astype(jnp.int32)
    level_shifts = []
    start = unique_count
    for rows in level_rows:
        level_shifts.append(shift_table[start : start + rows])
        start = start + rows

    base = jnp.sum(spectrogram.reshape(sub_dev, SUMMED, span_time), axis=1, dtype=jnp.float32)
    spread = jnp.broadcast_to(base[None], (tm_count,) + base.shape)
    gathered = lax.all_to_all(spread, "tm", 0, 0, tiled=True)
    base = jnp.transpose(gathered, (1, 0, 2)).reshape(sub_dev, tm_count * span_time)
    full_time = base.shape[1]
    local_limit = sum(2**k - 1 for k in range(1, sub_dev.bit_length()))
    moved = shift_rows(jnp.tile(base, (held, 1)), path_shift, max(local_limit.bit_length(), 1))
    trial_rows = jnp.sum(moved.reshape(held, sub_dev, full_time), axis=1)
    level = 0
    ready = None
    for bit_index in range(freq_bits):
        need_now = sub_dev * 2 ** (bit_index + 1) - 1
        if bit_index in groups:
            names, width = groups[bit_index]
            if ready is None:
                spread = jnp.broadcast_to(trial_rows[None], (2**width,) + trial_rows.shape)
            else:
                spread = ready
            ready = None
            later = groups.get(bit_index + width)
            peers = lax.all_to_all(spread, names, 0, 0, tiled=True)
            sets = [peers[index] for index in range(2**width)]
            for step in range(width):
                need_now = sub_dev * 2 ** (bit_index + step + 1) - 1
                if bit_index + step >= freq_bits - shared:
                    sets = [jnp.repeat(one, 2, axis=0) for one in sets]
                rows = sets[0].shape[0]
                last = step == width - 1 and later is not None
                merged = merge_rows(
                    jnp.concatenate(sets[0::2], axis=0),
                    zero_front(jnp.concatenate(sets[1::2], axis=0), need_now),
                    level_shifts[level],
                    need_now,
                    2 ** later[1] if last else 0,
                )
                if last:
                    ready = merged
                    merged = merged[0]
                sets = [merged[index * rows : (index + 1) * rows] for index in range(len(sets) // 2)]
                level = level + 1
            trial_rows = sets[0]
            continue
        if any(0 < bit_index - first < groups[first][1] for first in groups):
            continue
        if bit_index == freq_bits - 1 and shared >= 3 and bit_index >= 2:
            partner = paired(trial_rows, freq_axis, near_half(bit_index, bit_index - 2))
        else:
            partner = swapped(trial_rows, freq_axis, bit_index)
        upper_half = device >> bit_index & 1
        low_rows = jnp.where(upper_half == 1, partner, trial_rows)
        high_rows = jnp.where(upper_half == 1, trial_rows, partner)
        if bit_index >= freq_bits - shared:
            low_rows = jnp.repeat(low_rows, 2, axis=0)
            high_rows = jnp.repeat(high_rows, 2, axis=0)
        later = groups.get(bit_index + 1)
        trial_rows = merge_rows(
            low_rows, zero_front(high_rows, need_now), level_shifts[level], need_now,
            2 ** later[1] if later is not None else 0,
        )
        if later is not None:
            ready = trial_rows
            trial_rows = trial_rows[0]
        level = level + 1
    signal = trial_rows / math.sqrt(all_trials * SUMMED)
    peak_rows = []
    window_sum = signal
    width_now = 1
    for level_index in range(WIDTHS):
        peak_rows.append(jnp.max(window_sum, axis=0) / math.sqrt(width_now))
        if level_index + 1 < WIDTHS:
            window_sum = window_sum + zero_front(window_sum, width_now)[:, :full_time]
            width_now = width_now * 2
    best = jnp.stack(peak_rows).reshape(WIDTHS, tm_count, span_time)
    best = jnp.max(lax.all_to_all(best, "tm", 1, 1, tiled=True), axis=1)
    ready = None
    for bit_index in range(freq_bits - shared):
        if bit_index == 0 and "zl" in freq_axis and freq_bits - shared >= 4:
            partner = swapped(best, freq_axis, bit_index)
            stretch = lambda one: jnp.broadcast_to(one[None], (8,) + one.shape)
            ready = jnp.maximum(stretch(best), stretch(partner))
            best = ready[0]
        elif bit_index == 1 and "zl" in freq_axis and freq_bits - shared >= 4:
            spread = jnp.broadcast_to(best[None], (8,) + best.shape) if ready is None else ready
            best = jnp.max(lax.all_to_all(spread, ("zh", "zl"), 0, 0, tiled=True), axis=0)
        elif bit_index in (2, 3) and "zl" in freq_axis and freq_bits - shared >= 4:
            continue
        elif bit_index == 1 and "zl" in freq_axis:
            spread = jnp.broadcast_to(best[None], (4,) + best.shape)
            best = jnp.max(lax.all_to_all(spread, "zl", 0, 0, tiled=True), axis=0)
        elif bit_index == 2 and "zl" in freq_axis:
            continue
        elif bit_index == 3:
            best = jnp.maximum(best, paired(best, freq_axis, near_half(bit_index, 1)))
        else:
            best = jnp.maximum(best, swapped(best, freq_axis, bit_index))
    return best


def solution(mesh):
    count = mesh.shape["freq"]
    if count == 128:
        freq_axis, sizes = ("yh", "yl", "zh", "zl", "fc"), (2, 4, 2, 4, 2)
    elif count == 16:
        freq_axis, sizes = ("zh", "zl", "fc"), (2, 4, 2)
    else:
        freq_axis, sizes = ("freq",), (count,)
    fine = jax.sharding.Mesh(
        mesh.devices.reshape(sizes + (mesh.shape["tm"],)), freq_axis + ("tm",)
    )
    placed = (P(freq_axis, "tm"), P(), P())
    return jax.shard_map(
        functools.partial(shards, freq_axis), mesh=fine, in_specs=placed,
        out_specs=P(None, "tm"), check_vma=False,
    )
```

```python
import functools
import math

import numpy as np
import jax
import jax.numpy as jnp
from jax import lax
from jax.sharding import PartitionSpec as P

SUMMED = 32
WIDTHS = 9
SHARED_LEVELS = 3
NEAR_HALF = (6, 7, 4, 5, 2, 3, 0, 1)
FINE_BITS = {"yh": 1, "yl": 2, "zh": 1, "zl": 2, "fc": 1}


def swapped(block, axis, apart):
    count = lax.axis_size(axis)
    route = []
    for low in range(count):
        high = low | 1 << apart
        if high != low and high < count:
            route += [(low, high), (high, low)]
    return lax.ppermute(block, axis, route)


def paired(block, axis, partner_of):
    return lax.ppermute(block, axis, [(partner_of(i), i) for i in range(lax.axis_size(axis))])


def near_half(bit_index, ring_bits):
    def partner_of(i):
        ring = i >> ring_bits & 7
        return i - (ring << ring_bits) + (NEAR_HALF[ring] << ring_bits)

    return partner_of


def zero_front(rows, width):
    return jnp.pad(rows, [(0, 0)] * (rows.ndim - 1) + [(width, 0)])


def merge_rows(low_rows, high_rows, shifts, need_now, copies=0):
    offsets = need_now - shifts
    bit_count = max(need_now.bit_length(), 1)
    moved = high_rows
    for bit_index in range(bit_count):
        step_size = 2**bit_index
        cols = moved.shape[-1]
        selected = (offsets >> bit_index & 1)[:, None] == 1
        moved = jnp.where(selected, moved[:, step_size:], moved[:, : cols - step_size])
    if copies:
        return jnp.broadcast_to(low_rows[None], (copies,) + low_rows.shape) + jnp.broadcast_to(
            moved[None], (copies,) + moved.shape
        )
    return low_rows + moved


def shift_rows(rows, shifts, bit_count):
    limit = 2**bit_count - 1
    offsets = limit - shifts
    moved = zero_front(rows, limit)
    for bit_index in range(bit_count):
        step_size = 2**bit_index
        cols = moved.shape[-1]
        selected = (offsets >> bit_index & 1)[:, None] == 1
        moved = jnp.where(selected, moved[:, step_size:], moved[:, : cols - step_size])
    return moved


def picked(table, index):
    hit = index[:, None] == jnp.arange(table.shape[0], dtype=jnp.int32)[None, :]
    return jnp.sum(jnp.where(hit, table[None, :], 0), axis=1)


def delay_plan(sub_dev, held, tm_bits, freq_bits, shared, all_trials, choice_bits):
    terms = 1 + tm_bits + freq_bits
    local_bits = sub_dev.bit_length() - 1
    held_bits = held.bit_length() - 1

    def held_trial(m, right):
        value = np.zeros(terms, np.int64)
        for p in range(held_bits + tm_bits):
            if p < right:
                continue
            if p < held_bits:
                value[0] += (m >> p & 1) << (p - right)
            else:
                value[1 + p - held_bits] += 1 << (p - right)
        return value

    ids, rates, jits = [], [], []
    slot = {}
    for k in range(1, local_bits + 1):
        trial_count = 2**k
        for m in range(held):
            trial = held_trial(m, local_bits - k)
            for g in range(sub_dev >> k):
                key = (k, g, tuple(trial))
                if key in slot:
                    continue
                slot[key] = len(ids)
                rate = np.zeros(terms, np.int64)
                rate[0] = all_trials // trial_count - 1 + g
                for bit in range(freq_bits):
                    rate[1 + tm_bits + bit] = (sub_dev >> k) << bit
                jit = trial.copy()
                jit[0] += trial_count - 2
                ids.append(trial)
                rates.append(rate)
                jits.append(jit)
    paths = np.zeros((held * sub_dev, len(ids)), np.float32)
    for m in range(held):
        for i in range(sub_dev):
            for k in range(1, local_bits + 1):
                if i >> (k - 1) & 1:
                    key = (k, i >> k, tuple(held_trial(m, local_bits - k)))
                    paths[m * sub_dev + i, slot[key]] += 1.0
    unique_count = len(ids)
    level_rows = []
    now = np.zeros((held, terms), np.int64)
    for m in range(held):
        now[m] = held_trial(m, 0)
    for bit_index in range(freq_bits):
        trial_count = sub_dev * 2 ** (bit_index + 1)
        if bit_index >= freq_bits - shared:
            now = 2 * np.repeat(now, 2, axis=0)
            now[:, 0] = now[:, 0] + np.tile(np.arange(2), now.shape[0] // 2)
        else:
            now = 2 * now
            now[:, 1 + tm_bits + bit_index] = now[:, 1 + tm_bits + bit_index] + 1
        rate = np.zeros(terms, np.int64)
        rate[0] = all_trials // trial_count - 1
        for bit in range(bit_index + 1, freq_bits):
            rate[1 + tm_bits + bit] = 1 << (bit - bit_index - 1)
        choices = []
        spread_bits = choice_bits.get(bit_index, 0)
        for value in range(2**spread_bits):
            one = rate.copy()
            for step in range(spread_bits):
                one[1 + tm_bits + bit_index + 1 + step] = 0
            one[0] += value
            choices.append(one)
        for one in choices:
            for row in now:
                jit = row.copy()
                jit[0] += trial_count - 2
                ids.append(row.copy())
                rates.append(one)
                jits.append(jit)
        level_rows.append(now.shape[0] * len(choices))
    pack = lambda parts: np.stack(parts, axis=1).astype(np.int32)
    return pack(ids), pack(rates), pack(jits), paths, unique_count, level_rows


def shards(freq_axis, spectrogram, low_share, jitter):
    sub_dev = spectrogram.shape[0] // SUMMED
    span_time = spectrogram.shape[1]
    all_trials = low_share.shape[0] + 1
    freq_bits = lax.axis_size(freq_axis).bit_length() - 1
    tm_count = lax.axis_size("tm")
    shared = min(SHARED_LEVELS, freq_bits)
    device = lax.axis_index(freq_axis)
    place = lax.axis_index("tm")
    held = sub_dev // tm_count

    tm_bits = tm_count.bit_length() - 1
    groups = {}
    for first, names in ((1, ("zh", "zl")), (4, ("yl",))):
        width = sum(FINE_BITS[name] for name in names)
        redundant = {first + step >= freq_bits - shared for step in range(width)}
        if all(name in freq_axis for name in names) and len(redundant) == 1:
            groups[first] = (names, width)
    choice_bits = {}
    for first, (names, width) in groups.items():
        for step in range(width):
            choice_bits[first + step] = width - 1 - step
    id_terms, rate_terms, jitter_terms, paths, unique_count, level_rows = delay_plan(
        sub_dev, held, tm_bits, freq_bits, shared, all_trials, choice_bits
    )
    factors = jnp.concatenate(
        [jnp.ones((1,), jnp.int32),
         (place >> jnp.arange(tm_bits, dtype=jnp.int32) & 1).astype(jnp.int32),
         (device >> jnp.arange(freq_bits, dtype=jnp.int32) & 1).astype(jnp.int32)]
    )[:, None]
    ids_all = jnp.sum(factors * id_terms, axis=0)
    rates = picked(low_share, jnp.sum(factors * rate_terms, axis=0))
    jitters = picked(jitter, jnp.sum(factors * jitter_terms, axis=0))
    shift_table = (ids_all * rates + jitters) // 64
    path_shift = jnp.dot(
        paths, shift_table[:unique_count].astype(jnp.float32), precision=lax.Precision.HIGHEST
    )
    path_shift = jnp.round(path_shift).astype(jnp.int32)
    level_shifts = []
    start = unique_count
    for rows in level_rows:
        level_shifts.append(shift_table[start : start + rows])
        start = start + rows

    members = np.arange(sub_dev * SUMMED) // SUMMED == np.arange(sub_dev)[:, None]
    base = jnp.dot(
        jnp.asarray(members, jnp.bfloat16), spectrogram, preferred_element_type=jnp.float32
    )
    spread = jnp.broadcast_to(base[None], (tm_count,) + base.shape)
    gathered = lax.all_to_all(spread, "tm", 0, 0, tiled=True)
    base = jnp.transpose(gathered, (1, 0, 2)).reshape(sub_dev, tm_count * span_time)
    full_time = base.shape[1]
    local_limit = sum(2**k - 1 for k in range(1, sub_dev.bit_length()))
    moved = shift_rows(jnp.tile(base, (held, 1)), path_shift, max(local_limit.bit_length(), 1))
    trial_rows = jnp.sum(moved.reshape(held, sub_dev, full_time), axis=1)
    level = 0
    ready = None
    for bit_index in range(freq_bits):
        need_now = sub_dev * 2 ** (bit_index + 1) - 1
        if bit_index in groups:
            names, width = groups[bit_index]
            if ready is None:
                spread = jnp.broadcast_to(trial_rows[None], (2**width,) + trial_rows.shape)
            else:
                spread = ready
            ready = None
            later = groups.get(bit_index + width)
            peers = lax.all_to_all(spread, names, 0, 0, tiled=True)
            sets = [peers[index] for index in range(2**width)]
            for step in range(width):
                need_now = sub_dev * 2 ** (bit_index + step + 1) - 1
                if bit_index + step >= freq_bits - shared:
                    sets = [jnp.repeat(one, 2, axis=0) for one in sets]
                rows = sets[0].shape[0]
                last = step == width - 1 and later is not None
                merged = merge_rows(
                    jnp.concatenate(sets[0::2], axis=0),
                    zero_front(jnp.concatenate(sets[1::2], axis=0), need_now),
                    level_shifts[level],
                    need_now,
                    2 ** later[1] if last else 0,
                )
                if last:
                    ready = merged
                    merged = merged[0]
                sets = [merged[index * rows : (index + 1) * rows] for index in range(len(sets) // 2)]
                level = level + 1
            trial_rows = sets[0]
            continue
        if any(0 < bit_index - first < groups[first][1] for first in groups):
            continue
        if bit_index == freq_bits - 1 and shared >= 3 and bit_index >= 2:
            partner = paired(trial_rows, freq_axis, near_half(bit_index, bit_index - 2))
        else:
            partner = swapped(trial_rows, freq_axis, bit_index)
        upper_half = device >> bit_index & 1
        low_rows = jnp.where(upper_half == 1, partner, trial_rows)
        high_rows = jnp.where(upper_half == 1, trial_rows, partner)
        if bit_index >= freq_bits - shared:
            low_rows = jnp.repeat(low_rows, 2, axis=0)
            high_rows = jnp.repeat(high_rows, 2, axis=0)
        later = groups.get(bit_index + 1)
        trial_rows = merge_rows(
            low_rows, zero_front(high_rows, need_now), level_shifts[level], need_now,
            2 ** later[1] if later is not None else 0,
        )
        if later is not None:
            ready = trial_rows
            trial_rows = trial_rows[0]
        level = level + 1
    signal = trial_rows / math.sqrt(all_trials * SUMMED)
    peak_rows = []
    window_sum = signal
    width_now = 1
    for level_index in range(WIDTHS):
        peak_rows.append(jnp.max(window_sum, axis=0) / math.sqrt(width_now))
        if level_index + 1 < WIDTHS:
            window_sum = window_sum + zero_front(window_sum, width_now)[:, :full_time]
            width_now = width_now * 2
    best = jnp.stack(peak_rows).reshape(WIDTHS, tm_count, span_time)
    best = jnp.max(lax.all_to_all(best, "tm", 1, 1, tiled=True), axis=1)
    ready = None
    for bit_index in range(freq_bits - shared):
        if bit_index == 0 and "zl" in freq_axis and freq_bits - shared >= 4:
            partner = swapped(best, freq_axis, bit_index)
            stretch = lambda one: jnp.broadcast_to(one[None], (8,) + one.shape)
            ready = jnp.maximum(stretch(best), stretch(partner))
            best = ready[0]
        elif bit_index == 1 and "zl" in freq_axis and freq_bits - shared >= 4:
            spread = jnp.broadcast_to(best[None], (8,) + best.shape) if ready is None else ready
            best = jnp.max(lax.all_to_all(spread, ("zh", "zl"), 0, 0, tiled=True), axis=0)
        elif bit_index in (2, 3) and "zl" in freq_axis and freq_bits - shared >= 4:
            continue
        elif bit_index == 1 and "zl" in freq_axis:
            spread = jnp.broadcast_to(best[None], (4,) + best.shape)
            best = jnp.max(lax.all_to_all(spread, "zl", 0, 0, tiled=True), axis=0)
        elif bit_index == 2 and "zl" in freq_axis:
            continue
        elif bit_index == 3:
            best = jnp.maximum(best, paired(best, freq_axis, near_half(bit_index, 1)))
        else:
            best = jnp.maximum(best, swapped(best, freq_axis, bit_index))
    return best


def solution(mesh):
    count = mesh.shape["freq"]
    if count == 128:
        freq_axis, sizes = ("yh", "yl", "zh", "zl", "fc"), (2, 4, 2, 4, 2)
    elif count == 16:
        freq_axis, sizes = ("zh", "zl", "fc"), (2, 4, 2)
    else:
        freq_axis, sizes = ("freq",), (count,)
    fine = jax.sharding.Mesh(
        mesh.devices.reshape(sizes + (mesh.shape["tm"],)), freq_axis + ("tm",)
    )
    placed = (P(freq_axis, "tm"), P(), P())
    return jax.shard_map(
        functools.partial(shards, freq_axis), mesh=fine, in_specs=placed,
        out_specs=P(None, "tm"), check_vma=False,
    )
```

```python
import functools
import math

import numpy as np
import jax
import jax.numpy as jnp
from jax import lax
from jax.sharding import PartitionSpec as P

SUMMED = 32
WIDTHS = 9
SHARED_LEVELS = 3
NEAR_HALF = (6, 7, 4, 5, 2, 3, 0, 1)
FINE_BITS = {"yh": 1, "yl": 2, "zh": 1, "zl": 2, "fc": 1}


def swapped(block, axis, apart):
    count = lax.axis_size(axis)
    route = []
    for low in range(count):
        high = low | 1 << apart
        if high != low and high < count:
            route += [(low, high), (high, low)]
    return lax.ppermute(block, axis, route)


def paired(block, axis, partner_of):
    return lax.ppermute(block, axis, [(partner_of(i), i) for i in range(lax.axis_size(axis))])


def near_half(bit_index, ring_bits):
    def partner_of(i):
        ring = i >> ring_bits & 7
        return i - (ring << ring_bits) + (NEAR_HALF[ring] << ring_bits)

    return partner_of


def zero_front(rows, width):
    return jnp.pad(rows, [(0, 0)] * (rows.ndim - 1) + [(width, 0)])


def merge_rows(low_rows, high_rows, shifts, need_now, copies=0):
    offsets = need_now - shifts
    bit_count = max(need_now.bit_length(), 1)
    moved = high_rows
    for bit_index in range(bit_count):
        step_size = 2**bit_index
        cols = moved.shape[-1]
        selected = (offsets >> bit_index & 1)[:, None] == 1
        moved = jnp.where(selected, moved[:, step_size:], moved[:, : cols - step_size])
    if copies:
        return jnp.broadcast_to(low_rows[None], (copies,) + low_rows.shape) + jnp.broadcast_to(
            moved[None], (copies,) + moved.shape
        )
    return low_rows + moved


def shift_rows(rows, shifts, bit_count):
    limit = 2**bit_count - 1
    offsets = limit - shifts
    moved = zero_front(rows, limit)
    for bit_index in range(bit_count):
        step_size = 2**bit_index
        cols = moved.shape[-1]
        selected = (offsets >> bit_index & 1)[:, None] == 1
        moved = jnp.where(selected, moved[:, step_size:], moved[:, : cols - step_size])
    return moved


def picked(table, index):
    hit = index[:, None] == jnp.arange(table.shape[0], dtype=jnp.int32)[None, :]
    return jnp.sum(jnp.where(hit, table[None, :], 0), axis=1)


def delay_plan(sub_dev, held, tm_bits, freq_bits, shared, all_trials, choice_bits):
    terms = 1 + tm_bits + freq_bits
    local_bits = sub_dev.bit_length() - 1
    held_bits = held.bit_length() - 1

    def held_trial(m, right):
        value = np.zeros(terms, np.int64)
        for p in range(held_bits + tm_bits):
            if p < right:
                continue
            if p < held_bits:
                value[0] += (m >> p & 1) << (p - right)
            else:
                value[1 + p - held_bits] += 1 << (p - right)
        return value

    ids, rates, jits = [], [], []
    slot = {}
    for k in range(1, local_bits + 1):
        trial_count = 2**k
        for m in range(held):
            trial = held_trial(m, local_bits - k)
            for g in range(sub_dev >> k):
                key = (k, g, tuple(trial))
                if key in slot:
                    continue
                slot[key] = len(ids)
                rate = np.zeros(terms, np.int64)
                rate[0] = all_trials // trial_count - 1 + g
                for bit in range(freq_bits):
                    rate[1 + tm_bits + bit] = (sub_dev >> k) << bit
                jit = trial.copy()
                jit[0] += trial_count - 2
                ids.append(trial)
                rates.append(rate)
                jits.append(jit)
    paths = np.zeros((held * sub_dev, len(ids)), np.float32)
    for m in range(held):
        for i in range(sub_dev):
            for k in range(1, local_bits + 1):
                if i >> (k - 1) & 1:
                    key = (k, i >> k, tuple(held_trial(m, local_bits - k)))
                    paths[m * sub_dev + i, slot[key]] += 1.0
    unique_count = len(ids)
    level_rows = []
    now = np.zeros((held, terms), np.int64)
    for m in range(held):
        now[m] = held_trial(m, 0)
    for bit_index in range(freq_bits):
        trial_count = sub_dev * 2 ** (bit_index + 1)
        if bit_index >= freq_bits - shared:
            now = 2 * np.repeat(now, 2, axis=0)
            now[:, 0] = now[:, 0] + np.tile(np.arange(2), now.shape[0] // 2)
        else:
            now = 2 * now
            now[:, 1 + tm_bits + bit_index] = now[:, 1 + tm_bits + bit_index] + 1
        rate = np.zeros(terms, np.int64)
        rate[0] = all_trials // trial_count - 1
        for bit in range(bit_index + 1, freq_bits):
            rate[1 + tm_bits + bit] = 1 << (bit - bit_index - 1)
        choices = []
        spread_bits = choice_bits.get(bit_index, 0)
        for value in range(2**spread_bits):
            one = rate.copy()
            for step in range(spread_bits):
                one[1 + tm_bits + bit_index + 1 + step] = 0
            one[0] += value
            choices.append(one)
        for one in choices:
            for row in now:
                jit = row.copy()
                jit[0] += trial_count - 2
                ids.append(row.copy())
                rates.append(one)
                jits.append(jit)
        level_rows.append(now.shape[0] * len(choices))
    pack = lambda parts: np.stack(parts, axis=1).astype(np.int32)
    return pack(ids), pack(rates), pack(jits), paths, unique_count, level_rows


def shards(freq_axis, spectrogram, low_share, jitter):
    sub_dev = spectrogram.shape[0] // SUMMED
    span_time = spectrogram.shape[1]
    all_trials = low_share.shape[0] + 1
    freq_bits = lax.axis_size(freq_axis).bit_length() - 1
    tm_count = lax.axis_size("tm")
    shared = min(SHARED_LEVELS, freq_bits)
    device = lax.axis_index(freq_axis)
    place = lax.axis_index("tm")
    held = sub_dev // tm_count

    tm_bits = tm_count.bit_length() - 1
    groups = {}
    for first, names in ((1, ("zh", "zl")), (4, ("yl",))):
        width = sum(FINE_BITS[name] for name in names)
        redundant = {first + step >= freq_bits - shared for step in range(width)}
        if all(name in freq_axis for name in names) and len(redundant) == 1:
            groups[first] = (names, width)
    choice_bits = {}
    for first, (names, width) in groups.items():
        for step in range(width):
            choice_bits[first + step] = width - 1 - step
    id_terms, rate_terms, jitter_terms, paths, unique_count, level_rows = delay_plan(
        sub_dev, held, tm_bits, freq_bits, shared, all_trials, choice_bits
    )
    factors = jnp.concatenate(
        [jnp.ones((1,), jnp.int32),
         (place >> jnp.arange(tm_bits, dtype=jnp.int32) & 1).astype(jnp.int32),
         (device >> jnp.arange(freq_bits, dtype=jnp.int32) & 1).astype(jnp.int32)]
    )[:, None]
    ids_all = jnp.sum(factors * id_terms, axis=0)
    rates = picked(low_share, jnp.sum(factors * rate_terms, axis=0))
    jitters = picked(jitter, jnp.sum(factors * jitter_terms, axis=0))
    shift_table = (ids_all * rates + jitters) // 64
    path_shift = jnp.dot(
        paths, shift_table[:unique_count].astype(jnp.float32), precision=lax.Precision.HIGHEST
    )
    path_shift = jnp.round(path_shift).astype(jnp.int32)
    level_shifts = []
    start = unique_count
    for rows in level_rows:
        level_shifts.append(shift_table[start : start + rows])
        start = start + rows

    base = jnp.sum(spectrogram.reshape(sub_dev, SUMMED, span_time), axis=1, dtype=jnp.float32)
    spread = jnp.broadcast_to(base[None], (tm_count,) + base.shape)
    gathered = lax.all_to_all(spread, "tm", 0, 0, tiled=True)
    base = jnp.transpose(gathered, (1, 0, 2)).reshape(sub_dev, tm_count * span_time)
    full_time = base.shape[1]
    local_limit = sum(2**k - 1 for k in range(1, sub_dev.bit_length()))
    moved = shift_rows(jnp.tile(base, (held, 1)), path_shift, max(local_limit.bit_length(), 1))
    trial_rows = jnp.sum(moved.reshape(held, sub_dev, full_time), axis=1)
    level = 0
    ready = None
    for bit_index in range(freq_bits):
        need_now = sub_dev * 2 ** (bit_index + 1) - 1
        if bit_index in groups:
            names, width = groups[bit_index]
            if ready is None:
                spread = jnp.broadcast_to(trial_rows[None], (2**width,) + trial_rows.shape)
            else:
                spread = ready
            ready = None
            later = groups.get(bit_index + width)
            peers = lax.all_to_all(spread, names, 0, 0, tiled=True)
            sets = [peers[index] for index in range(2**width)]
            for step in range(width):
                need_now = sub_dev * 2 ** (bit_index + step + 1) - 1
                if bit_index + step >= freq_bits - shared:
                    sets = [jnp.repeat(one, 2, axis=0) for one in sets]
                rows = sets[0].shape[0]
                last = step == width - 1 and later is not None
                merged = merge_rows(
                    jnp.concatenate(sets[0::2], axis=0),
                    zero_front(jnp.concatenate(sets[1::2], axis=0), need_now),
                    level_shifts[level],
                    need_now,
                    2 ** later[1] if last else 0,
                )
                if last:
                    ready = merged
                    merged = merged[0]
                sets = [merged[index * rows : (index + 1) * rows] for index in range(len(sets) // 2)]
                level = level + 1
            trial_rows = sets[0]
            continue
        if any(0 < bit_index - first < groups[first][1] for first in groups):
            continue
        if bit_index == freq_bits - 1 and shared >= 3 and bit_index >= 2:
            partner = paired(trial_rows, freq_axis, near_half(bit_index, bit_index - 2))
        else:
            partner = swapped(trial_rows, freq_axis, bit_index)
        upper_half = device >> bit_index & 1
        low_rows = jnp.where(upper_half == 1, partner, trial_rows)
        high_rows = jnp.where(upper_half == 1, trial_rows, partner)
        if bit_index >= freq_bits - shared:
            low_rows = jnp.repeat(low_rows, 2, axis=0)
            high_rows = jnp.repeat(high_rows, 2, axis=0)
        later = groups.get(bit_index + 1)
        trial_rows = merge_rows(
            low_rows, zero_front(high_rows, need_now), level_shifts[level], need_now,
            2 ** later[1] if later is not None else 0,
        )
        if later is not None:
            ready = trial_rows
            trial_rows = trial_rows[0]
        level = level + 1
    signal = trial_rows
    peak_rows = []
    window_sum = signal
    width_now = 1
    for level_index in range(WIDTHS):
        peak_rows.append(jnp.max(window_sum, axis=0) / math.sqrt(all_trials * SUMMED) / math.sqrt(width_now))
        if level_index + 1 < WIDTHS:
            window_sum = window_sum + zero_front(window_sum, width_now)[:, :full_time]
            width_now = width_now * 2
    best = jnp.stack(peak_rows).reshape(WIDTHS, tm_count, span_time)
    best = jnp.max(lax.all_to_all(best, "tm", 1, 1, tiled=True), axis=1)
    ready = None
    for bit_index in range(freq_bits - shared):
        if bit_index == 0 and "zl" in freq_axis and freq_bits - shared >= 4:
            partner = swapped(best, freq_axis, bit_index)
            stretch = lambda one: jnp.broadcast_to(one[None], (8,) + one.shape)
            ready = jnp.maximum(stretch(best), stretch(partner))
            best = ready[0]
        elif bit_index == 1 and "zl" in freq_axis and freq_bits - shared >= 4:
            spread = jnp.broadcast_to(best[None], (8,) + best.shape) if ready is None else ready
            best = jnp.max(lax.all_to_all(spread, ("zh", "zl"), 0, 0, tiled=True), axis=0)
        elif bit_index in (2, 3) and "zl" in freq_axis and freq_bits - shared >= 4:
            continue
        elif bit_index == 1 and "zl" in freq_axis:
            spread = jnp.broadcast_to(best[None], (4,) + best.shape)
            best = jnp.max(lax.all_to_all(spread, "zl", 0, 0, tiled=True), axis=0)
        elif bit_index == 2 and "zl" in freq_axis:
            continue
        elif bit_index == 3:
            best = jnp.maximum(best, paired(best, freq_axis, near_half(bit_index, 1)))
        else:
            best = jnp.maximum(best, swapped(best, freq_axis, bit_index))
    return best


def solution(mesh):
    count = mesh.shape["freq"]
    if count == 128:
        freq_axis, sizes = ("yh", "yl", "zh", "zl", "fc"), (2, 4, 2, 4, 2)
    elif count == 16:
        freq_axis, sizes = ("zh", "zl", "fc"), (2, 4, 2)
    else:
        freq_axis, sizes = ("freq",), (count,)
    fine = jax.sharding.Mesh(
        mesh.devices.reshape(sizes + (mesh.shape["tm"],)), freq_axis + ("tm",)
    )
    placed = (P(freq_axis, "tm"), P(), P())
    return jax.shard_map(
        functools.partial(shards, freq_axis), mesh=fine, in_specs=placed,
        out_specs=P(None, "tm"), check_vma=False,
    )
```
